128 devices in a mesh: ctx: 16 (over x_lo, z, core), tp: 8 (over y, x_hi).
Axes of the slice: x: 4 (x_hi: 2, x_lo: 2; x = x_hi * 2 + x_lo), y: 4, z: 4, core: 2. Of those that a mesh axis runs over, the one named last changes fastest.
Arguments:
- queries: bfloat16 [8192, 4096], P('ctx', 'tp'), may hold values from -6 to 6
- key_rows: bfloat16 [8192, 4096], P('ctx', 'tp'), may hold values from -6 to 6
- value_rows: bfloat16 [8192, 4096], P('ctx', 'tp'), may hold values from -30 to 30
- selection: int32 [16, 3], replicated, may hold values from 0 to 15, as said below
- out_weight: bfloat16 [4096, 7168], P('tp'), may hold values from -0.125 to 0.125
Outputs:
- mixed: bfloat16 [8192, 7168], P('ctx', 'tp')
The draws below stay inside these ranges and needn't reach their ends.
Inputs may be any that keep to these rules, and one draw needn't show every extreme that they name: Row q of selection lists q first, then 3 - 1 distinct blocks below q; where fewer than that lie below q, the remaining entries are q.
All inputs are finite; a program needn't handle non-finite values.
Results may differ from the reference program's by a relative error of at most 0.013.
Values may be sent and summed in bfloat16 or wider, within the bound.
No kernel may reach another device: no remote copies, remote signals or barrier semaphores. Data moves between devices by JAX's collectives and lax.ppermute only.
A program may use at most 192 MiB of HBM per device.

```python
import jax
import jax.numpy as jnp
from jax import lax

D = 7168
HD = 128
BLOCK = 512
TOPK = 3
HEADS = 32
NB = 16
TOKENS = 8192


def paired_rows(key):
    base = jax.random.fold_in(key, 7)
    key_query, key_keys = jax.random.split(base, 2)
    shape = (TOKENS, HEADS * HD)
    query_vals = jnp.clip(1.3 * jax.random.normal(key_query, shape, jnp.float32), -6.0, 6.0)
    key_vals = jnp.clip(1.3 * jax.random.normal(key_keys, shape, jnp.float32), -6.0, 6.0)
    return (query_vals, key_vals)


def draw_queries(key, part):
    return paired_rows(key)[0].astype(jnp.bfloat16)


def draw_key_rows(key, part):
    return paired_rows(key)[1].astype(jnp.bfloat16)


def draw_selection(key, part):
    block_rows = jnp.arange(NB, dtype=jnp.int32)[:, None]
    block_cols = jnp.arange(NB, dtype=jnp.int32)[None, :]
    random_part = jax.random.randint(jax.random.fold_in(key, 3), (NB, NB), 0, 1 << 16)
    valid_score = random_part * NB + block_cols + NB
    other_score = NB - 1 - (block_cols - block_rows)
    scores = jnp.where(block_cols < block_rows, valid_score, other_score).astype(jnp.int32)
    _, picked = jax.lax.top_k(scores, TOPK - 1)
    picked = jnp.where(picked <= block_rows, picked, block_rows).astype(jnp.int32)
    return jnp.concatenate([block_rows, picked], axis=1).astype(jnp.int32)


def with_spikes(drawn, stream_key, source, target, blocks, factor):
    def block_of(dim):
        return (jnp.arange(drawn.shape[dim]) // (drawn.shape[dim] // blocks)).reshape((-1,) + (1,) * (drawn.ndim - 1 - dim))

    first = jax.random.permutation(stream_key, blocks)[block_of(target)]
    other_side = (block_of(target) + blocks // 2) % blocks
    return jnp.where((block_of(source) == first) | (block_of(source) == other_side), factor * drawn, drawn)


def block_scale(rng, shape, cuts, least, high):
    factor_of, own = 1.0, jax.random.fold_in(rng, 6)
    for position, blocks in cuts:
        draws = jnp.exp(jax.random.uniform(jax.random.fold_in(own, position), (blocks,), jnp.float32, least / len(cuts), high / len(cuts)))
        factor_of = factor_of * jnp.repeat(draws, shape[position] // blocks).reshape([-1 if axis == position else 1 for axis in range(len(shape))])
    return factor_of


def gaussian(own_key, shape, spread, reach, pieces=(), held_as=jnp.bfloat16):
    array = spread * jax.random.normal(own_key, shape, jnp.float32)
    if pieces:
        array = array * block_scale(own_key, shape, pieces, -0.22, 0.18)
    return jnp.clip(array, -reach, reach).astype(held_as)


def bell_draw_with(stream_key, dims, width, limit, cuts, heavy, kind=jnp.bfloat16):
    array = width * jax.random.normal(stream_key, dims, jnp.float32)
    if cuts:
        array = array * block_scale(stream_key, dims, cuts, -0.22, 0.18)
    return jnp.clip(with_spikes(array, jax.random.fold_in(stream_key, 3), *heavy), -limit, limit).astype(kind)


def setup_inputs(seed: int = 0) -> dict:
    streams_of = jax.random.split(jax.random.key(seed), 6)
    return {
        "queries": draw_queries(jax.random.fold_in(streams_of[5], 71), 0),
        "key_rows": draw_key_rows(jax.random.fold_in(streams_of[5], 71), 0),
        "value_rows": gaussian(streams_of[2], (TOKENS, HEADS * HD), 5.0, 30.0, ((0, 16), (1, 8))),
        "selection": draw_selection(jax.random.fold_in(streams_of[5], 71), 0),
        "out_weight": bell_draw_with(streams_of[4], (HEADS * HD, D), (HEADS * HD) ** -0.5, 0.125, ((0, 8),), (0, 1, 8, 2.0)),
    }


def reference(queries, key_rows, value_rows, selection, out_weight):
    query_blocks = queries.reshape(NB, BLOCK, HEADS, HD)
    key_blocks = key_rows.reshape(NB, BLOCK, HEADS, HD)
    value_blocks = value_rows.reshape(NB, BLOCK, HEADS, HD)
    scaling = 1.0 / jnp.sqrt(jnp.float32(HD))

    def block_out(block_index):
        listed = selection[block_index].astype(jnp.int32)
        repeated = jnp.concatenate([jnp.zeros((1,), bool), listed[1:] == listed[0]])
        picked_keys = jnp.take(key_blocks, listed, axis=0).reshape(TOPK * BLOCK, HEADS, HD)
        picked_values = jnp.take(value_blocks, listed, axis=0).reshape(TOPK * BLOCK, HEADS, HD)
        query_pos = block_index * BLOCK + jnp.arange(BLOCK, dtype=jnp.int32)
        key_pos = (listed[:, None] * BLOCK + jnp.arange(BLOCK, dtype=jnp.int32)[None, :]).reshape(-1)
        usable = jnp.repeat(jnp.logical_not(repeated), BLOCK)
        allowed = (key_pos[None, :] <= query_pos[:, None]) & usable[None, :]
        scores = jnp.einsum('thd,shd->hts', query_blocks[block_index].astype(jnp.float32), picked_keys.astype(jnp.float32)) * scaling
        row_max = lax.optimization_barrier(jnp.max(jnp.where(allowed[None], scores, -jnp.inf), axis=-1))
        expo = jnp.where(allowed[None], jnp.exp(scores - row_max[..., None]), 0.0)
        row_sum = lax.optimization_barrier(jnp.sum(expo, axis=-1))
        weights = lax.optimization_barrier(expo.astype(jnp.bfloat16))
        numer = jnp.einsum('hts,shd->thd', weights.astype(jnp.float32), picked_values.astype(jnp.float32))
        result = numer / jnp.transpose(row_sum)[..., None]
        return result.astype(jnp.bfloat16).reshape(BLOCK, HEADS * HD)
    attended = lax.map(block_out, jnp.arange(NB, dtype=jnp.int32)).reshape(TOKENS, HEADS * HD)
    return jnp.dot(attended, out_weight, preferred_element_type=jnp.float32).astype(jnp.bfloat16)
```

```python
import jax
import jax.numpy as jnp
from jax import lax
from jax.sharding import PartitionSpec as P

HD = 128
BLOCK = 512

neg_fill = -1e30


def per_device(queries, key_rows, value_rows, selection, out_weight):
    row_count, feat_width = queries.shape
    head_count = feat_width // HD
    topk = selection.shape[1]
    ctx_place = lax.axis_index("ctx")
    first_row = ctx_place * row_count
    scaling = 1.0 / jnp.sqrt(jnp.float32(HD))
    query_heads = queries.reshape(row_count, head_count, HD).transpose(1, 0, 2)
    own_choice = lax.dynamic_slice_in_dim(selection, ctx_place, 1, 0)[0]
    usable = jnp.concatenate([jnp.ones((1,), bool), own_choice[1:] != own_choice[0]])
    kv_piece = lax.all_gather(
        jnp.concatenate([key_rows, value_rows], axis=1), "ctx", axis=0, tiled=True
    )
    picked = jnp.stack(
        [lax.dynamic_slice_in_dim(kv_piece, own_choice[s] * BLOCK, BLOCK, 0) for s in range(topk)]
    ).reshape(topk * BLOCK, 2, head_count, HD)
    key_heads = picked[:, 0].transpose(1, 0, 2)
    value_heads = picked[:, 1].transpose(1, 0, 2)
    query_pos = first_row + jnp.arange(row_count, dtype=jnp.int32)
    key_pos = (own_choice[:, None] * BLOCK + jnp.arange(BLOCK, dtype=jnp.int32)[None, :]).reshape(-1)
    slot_ok = jnp.repeat(usable, BLOCK)
    allowed = (key_pos[None, :] <= query_pos[:, None]) & slot_ok[None, :]
    scores = (
        jnp.einsum("htd,hsd->hts", query_heads, key_heads, preferred_element_type=jnp.float32)
        * scaling
    )
    run_max = jnp.max(jnp.where(allowed[None], scores, neg_fill), axis=-1)
    expo = jnp.where(allowed[None], jnp.exp(scores - run_max[..., None]), 0.0)
    run_sum = jnp.sum(expo, axis=-1)
    weights = expo.astype(jnp.bfloat16)
    run_acc = jnp.einsum("hts,hsd->htd", weights, value_heads, preferred_element_type=jnp.float32)
    attended = (
        (run_acc / run_sum[..., None])
        .astype(jnp.bfloat16)
        .transpose(1, 0, 2)
        .reshape(row_count, feat_width)
    )
    shares = lax.psum_scatter(
        lax.dot_general(
            out_weight, attended, (((0,), (1,)), ((), ())), preferred_element_type=jnp.float32
        ).astype(jnp.bfloat16),
        "tp",
        scatter_dimension=0,
        tiled=True,
    ).astype(jnp.float32)
    mixed_out = jnp.transpose(shares)
    return mixed_out.astype(jnp.bfloat16)


def solution(mesh):
    placed = (P("ctx", "tp"), P("ctx", "tp"), P("ctx", "tp"), P(), P("tp", None))
    return jax.shard_map(
        per_device, mesh=mesh, in_specs=placed, out_specs=P("ctx", "tp"), check_vma=False
    )
```

```python
import jax
import jax.numpy as jnp
from jax import lax
from jax.sharding import PartitionSpec as P

HD = 128
BLOCK = 512

neg_fill = -1e30


def per_device(queries, key_rows, value_rows, selection, out_weight):
    row_count, feat_width = queries.shape
    head_count = feat_width // HD
    topk = selection.shape[1]
    ctx_place = lax.axis_index("ctx")
    first_row = ctx_place * row_count
    scaling = 1.0 / jnp.sqrt(jnp.float32(HD))
    query_heads = queries.reshape(row_count, head_count, HD).transpose(1, 0, 2)
    own_choice = lax.dynamic_slice_in_dim(selection, ctx_place, 1, 0)[0]
    usable = jnp.concatenate([jnp.ones((1,), bool), own_choice[1:] != own_choice[0]])
    kv_piece = lax.all_gather(
        jnp.concatenate([key_rows, value_rows], axis=1), "ctx", axis=0, tiled=True
    )
    tp_size = lax.axis_size("tp")
    tp_place = lax.axis_index("tp")
    col_width = out_weight.shape[1] // tp_size
    w_cols = jnp.zeros((out_weight.shape[0] * tp_size, col_width), out_weight.dtype)
    w_cols = lax.dynamic_update_slice_in_dim(
        w_cols,
        lax.dynamic_slice_in_dim(out_weight, tp_place * col_width, col_width, 1),
        tp_place * out_weight.shape[0],
        0,
    )
    for shift in range(1, tp_size):
        dest = (tp_place + shift) % tp_size
        sent = lax.dynamic_slice_in_dim(out_weight, dest * col_width, col_width, 1)
        got = lax.ppermute(sent, "tp", [(i, (i + shift) % tp_size) for i in range(tp_size)])
        src = (tp_place - shift) % tp_size
        w_cols = lax.dynamic_update_slice_in_dim(w_cols, got, src * out_weight.shape[0], 0)
    kv_piece, w_cols = lax.optimization_barrier((kv_piece, w_cols))
    picked = jnp.stack(
        [lax.dynamic_slice_in_dim(kv_piece, own_choice[s] * BLOCK, BLOCK, 0) for s in range(topk)]
    ).reshape(topk * BLOCK, 2, head_count, HD)
    key_heads = picked[:, 0].transpose(1, 0, 2)
    value_heads = picked[:, 1].transpose(1, 0, 2)
    query_pos = first_row + jnp.arange(row_count, dtype=jnp.int32)
    key_pos = (own_choice[:, None] * BLOCK + jnp.arange(BLOCK, dtype=jnp.int32)[None, :]).reshape(-1)
    slot_ok = jnp.repeat(usable, BLOCK)
    allowed = (key_pos[None, :] <= query_pos[:, None]) & slot_ok[None, :]
    scores = (
        jnp.einsum("htd,hsd->hts", query_heads, key_heads, preferred_element_type=jnp.float32)
        * scaling
    )
    run_max = jnp.max(jnp.where(allowed[None], scores, neg_fill), axis=-1)
    expo = jnp.where(allowed[None], jnp.exp(scores - run_max[..., None]), 0.0)
    run_sum = jnp.sum(expo, axis=-1)
    weights = expo.astype(jnp.bfloat16)
    run_acc = jnp.einsum("hts,hsd->htd", weights, value_heads, preferred_element_type=jnp.float32)
    attended = (
        (run_acc / run_sum[..., None])
        .astype(jnp.bfloat16)
        .transpose(1, 0, 2)
        .reshape(row_count, feat_width)
    )
    att_full = lax.all_gather(attended, "tp", axis=1, tiled=True)
    mixed_out = jnp.dot(att_full, w_cols, preferred_element_type=jnp.float32)
    return mixed_out.astype(jnp.bfloat16)


def solution(mesh):
    placed = (P("ctx", "tp"), P("ctx", "tp"), P("ctx", "tp"), P(), P("tp", None))
    return jax.shard_map(
        per_device, mesh=mesh, in_specs=placed, out_specs=P("ctx", "tp"), check_vma=False
    )
```

```python
import functools

import jax
import jax.numpy as jnp
from jax import lax
from jax.experimental import pallas as pl
from jax.experimental.pallas import tpu as pltpu
from jax.sharding import PartitionSpec as P

HD = 128
BLOCK = 512

neg_fill = -1e30


def attend_kernel(meta_ref, q_ref, k0_ref, k1_ref, k2_ref, v0_ref, v1_ref, v2_ref, o_ref, *, topk):
    scaling = 1.0 / jnp.sqrt(jnp.float32(HD))
    q = q_ref[...]
    query_pos = meta_ref[topk] * BLOCK + lax.broadcasted_iota(jnp.int32, (BLOCK, BLOCK), 0)
    key_off = lax.broadcasted_iota(jnp.int32, (BLOCK, BLOCK), 1)
    k_refs = (k0_ref, k1_ref, k2_ref)
    v_refs = (v0_ref, v1_ref, v2_ref)
    scores = []
    masks = []
    for s in range(topk):
        sc = lax.dot_general(
            q, k_refs[s][...], (((1,), (1,)), ((), ())), preferred_element_type=jnp.float32
        ) * scaling
        ok = (meta_ref[s] * BLOCK + key_off) <= query_pos
        if s > 0:
            ok = ok & (meta_ref[s] != meta_ref[0])
        scores.append(sc)
        masks.append(ok)
    row_max = jnp.max(jnp.where(masks[0], scores[0], neg_fill), axis=1, keepdims=True)
    for s in range(1, topk):
        row_max = jnp.maximum(
            row_max, jnp.max(jnp.where(masks[s], scores[s], neg_fill), axis=1, keepdims=True)
        )
    row_sum = jnp.zeros((BLOCK, 1), jnp.float32)
    acc = jnp.zeros((BLOCK, HD), jnp.float32)
    for s in range(topk):
        e = jnp.where(masks[s], jnp.exp(scores[s] - row_max), 0.0)
        row_sum = row_sum + jnp.sum(e, axis=1, keepdims=True)
        acc = acc + jnp.dot(
            e.astype(jnp.bfloat16), v_refs[s][...], preferred_element_type=jnp.float32
        )
    o_ref[...] = (acc / row_sum).astype(o_ref.dtype)


def attend(meta, queries, kv_piece, head_count, topk):
    def k_map(s):
        return lambda h, m: (m[s], h)

    def v_map(s):
        return lambda h, m: (m[s], head_count + h)

    blk = (BLOCK, HD)
    grid_spec = pltpu.PrefetchScalarGridSpec(
        num_scalar_prefetch=1,
        grid=(head_count,),
        in_specs=[pl.BlockSpec(blk, lambda h, m: (0, h))]
        + [pl.BlockSpec(blk, k_map(s)) for s in range(topk)]
        + [pl.BlockSpec(blk, v_map(s)) for s in range(topk)],
        out_specs=pl.BlockSpec(blk, lambda h, m: (0, h)),
    )
    return pl.pallas_call(
        functools.partial(attend_kernel, topk=topk),
        grid_spec=grid_spec,
        out_shape=jax.ShapeDtypeStruct(queries.shape, queries.dtype),
        cost_estimate=pl.CostEstimate(
            flops=4 * head_count * BLOCK * topk * BLOCK * HD,
            transcendentals=head_count * BLOCK * topk * BLOCK,
            bytes_accessed=2 * queries.size * 2 + 2 * topk * BLOCK * head_count * HD * 2,
        ),
    )(meta, queries, *([kv_piece] * (2 * topk)))


def per_device(queries, key_rows, value_rows, selection, out_weight):
    row_count, feat_width = queries.shape
    head_count = feat_width // HD
    topk = selection.shape[1]
    tp_size = lax.axis_size("tp")
    ctx_place = lax.axis_index("ctx")
    own_choice = lax.dynamic_slice_in_dim(selection, ctx_place, 1, 0)[0]
    meta = jnp.concatenate([own_choice, ctx_place.astype(jnp.int32)[None]])
    kv_piece = lax.all_gather(
        jnp.concatenate([key_rows, value_rows], axis=1), "ctx", axis=0, tiled=True
    )
    attended = attend(meta, queries, kv_piece, head_count, topk)
    col_width = out_weight.shape[1] // tp_size
    partial = jnp.einsum(
        "tk,kjc->jtc",
        attended,
        out_weight.reshape(out_weight.shape[0], tp_size, col_width),
        preferred_element_type=jnp.float32,
    ).astype(jnp.bfloat16)
    shares = lax.psum_scatter(partial, "tp", scatter_dimension=0, tiled=True)
    return shares.reshape(row_count, col_width)


def solution(mesh):
    placed = (P("ctx", "tp"), P("ctx", "tp"), P("ctx", "tp"), P(), P("tp", None))
    return jax.shard_map(
        per_device, mesh=mesh, in_specs=placed, out_specs=P("ctx", "tp"), check_vma=False
    )
```

```python
import functools

import jax
import jax.numpy as jnp
from jax import lax
from jax.experimental import pallas as pl
from jax.experimental.pallas import tpu as pltpu
from jax.sharding import PartitionSpec as P

HD = 128
BLOCK = 512

neg_fill = -1e30


def layer_kernel(meta_ref, q_ref, *refs, topk, head_count):
    k_refs = refs[:topk]
    v_refs = refs[topk : 2 * topk]
    w_ref, o_ref, att_ref = refs[2 * topk :]

    @pl.when(pl.program_id(0) == 0)
    def _():
        scaling = 1.0 / jnp.sqrt(jnp.float32(HD))
        q_block = meta_ref[topk]
        query_pos = q_block * BLOCK + lax.broadcasted_iota(jnp.int32, (BLOCK, BLOCK), 0)
        key_pos = meta_ref[0] * BLOCK + lax.broadcasted_iota(jnp.int32, (BLOCK, BLOCK), 1)
        causal = key_pos <= query_pos
        usable = [None] + [
            (meta_ref[s] != meta_ref[0]) & (meta_ref[s] < q_block) for s in range(1, topk)
        ]
        for h in range(head_count):
            cols = slice(h * HD, (h + 1) * HD)
            q = q_ref[:, cols]
            scores = []
            for s in range(topk):
                sc = lax.dot_general(
                    q, k_refs[s][:, cols], (((1,), (1,)), ((), ())),
                    preferred_element_type=jnp.float32,
                ) * scaling
                if s == 0:
                    sc = jnp.where(causal, sc, neg_fill)
                else:
                    sc = jnp.where(usable[s], sc, neg_fill)
                scores.append(sc)
            row_max = jnp.max(scores[0], axis=1, keepdims=True)
            for s in range(1, topk):
                row_max = jnp.maximum(row_max, jnp.max(scores[s], axis=1, keepdims=True))
            row_sum = jnp.zeros((BLOCK, 1), jnp.float32)
            acc = jnp.zeros((BLOCK, HD), jnp.float32)
            for s in range(topk):
                e = jnp.exp(scores[s] - row_max)
                row_sum = row_sum + jnp.sum(e, axis=1, keepdims=True)
                acc = acc + jnp.dot(
                    e.astype(jnp.bfloat16), v_refs[s][:, cols],
                    preferred_element_type=jnp.float32,
                )
            att_ref[:, cols] = (acc / row_sum).astype(att_ref.dtype)

    o_ref[0] = jnp.dot(att_ref[...], w_ref[...], preferred_element_type=jnp.float32).astype(
        o_ref.dtype
    )


def layer(meta, queries, kv_piece, out_weight, topk, chunks):
    row_count, feat_width = queries.shape
    head_count = feat_width // HD
    col_width = out_weight.shape[1] // chunks

    def k_map(s):
        return lambda j, m: (m[s], 0)

    def v_map(s):
        return lambda j, m: (m[s], 1)

    blk = (BLOCK, feat_width)
    grid_spec = pltpu.PrefetchScalarGridSpec(
        num_scalar_prefetch=1,
        grid=(chunks,),
        in_specs=[pl.BlockSpec(blk, lambda j, m: (0, 0))]
        + [pl.BlockSpec(blk, k_map(s)) for s in range(topk)]
        + [pl.BlockSpec(blk, v_map(s)) for s in range(topk)]
        + [pl.BlockSpec((out_weight.shape[0], col_width), lambda j, m: (0, j))],
        out_specs=pl.BlockSpec((1, row_count, col_width), lambda j, m: (j, 0, 0)),
        scratch_shapes=[pltpu.VMEM((row_count, feat_width), queries.dtype)],
    )
    attn_flops = 4 * head_count * BLOCK * topk * BLOCK * HD
    proj_flops = 2 * row_count * feat_width * out_weight.shape[1]
    return pl.pallas_call(
        functools.partial(layer_kernel, topk=topk, head_count=head_count),
        grid_spec=grid_spec,
        out_shape=jax.ShapeDtypeStruct((chunks, row_count, col_width), queries.dtype),
        compiler_params=pltpu.CompilerParams(dimension_semantics=("arbitrary",)),
        cost_estimate=pl.CostEstimate(
            flops=attn_flops + proj_flops,
            transcendentals=head_count * BLOCK * topk * BLOCK,
            bytes_accessed=queries.size * 2 * (1 + 2 * topk) + out_weight.size * 2 * 2,
        ),
    )(meta, queries, *([kv_piece] * (2 * topk)), out_weight)


def per_device(queries, key_rows, value_rows, selection, out_weight):
    row_count, feat_width = queries.shape
    topk = selection.shape[1]
    tp_size = lax.axis_size("tp")
    ctx_place = lax.axis_index("ctx")
    own_choice = lax.dynamic_slice_in_dim(selection, ctx_place, 1, 0)[0]
    meta = jnp.concatenate([own_choice, ctx_place.astype(jnp.int32)[None]])
    kv_piece = lax.all_gather(
        jnp.concatenate([key_rows, value_rows], axis=1), "ctx", axis=0, tiled=True
    )
    partial = layer(meta, queries, kv_piece, out_weight, topk, tp_size)
    shares = lax.psum_scatter(partial, "tp", scatter_dimension=0, tiled=True)
    return shares.reshape(row_count, out_weight.shape[1] // tp_size)


def solution(mesh):
    placed = (P("ctx", "tp"), P("ctx", "tp"), P("ctx", "tp"), P(), P("tp", None))
    return jax.shard_map(
        per_device, mesh=mesh, in_specs=placed, out_specs=P("ctx", "tp"), check_vma=False
    )
```

```python
import functools

import jax
import jax.numpy as jnp
from jax import lax
from jax.experimental import pallas as pl
from jax.experimental.pallas import tpu as pltpu
from jax.sharding import Mesh, PartitionSpec as P

HD = 128
BLOCK = 512

neg_fill = -1e30


def attend_kernel(meta_ref, q_ref, *refs, topk, head_count):
    k_refs = refs[:topk]
    v_refs = refs[topk : 2 * topk]
    att_ref = refs[2 * topk]
    if True:
        scaling = 1.0 / jnp.sqrt(jnp.float32(HD))
        q_block = meta_ref[topk]
        query_pos = q_block * BLOCK + lax.broadcasted_iota(jnp.int32, (BLOCK, BLOCK), 0)
        key_pos = meta_ref[0] * BLOCK + lax.broadcasted_iota(jnp.int32, (BLOCK, BLOCK), 1)
        causal = key_pos <= query_pos
        usable = [None] + [
            (meta_ref[s] != meta_ref[0]) & (meta_ref[s] < q_block) for s in range(1, topk)
        ]
        for h in range(head_count):
            cols = slice(h * HD, (h + 1) * HD)
            q = q_ref[:, cols]
            scores = []
            for s in range(topk):
                sc = lax.dot_general(
                    q, k_refs[s][:, cols], (((1,), (1,)), ((), ())),
                    preferred_element_type=jnp.float32,
                ) * scaling
                if s == 0:
                    sc = jnp.where(causal, sc, neg_fill)
                else:
                    sc = jnp.where(usable[s], sc, neg_fill)
                scores.append(sc)
            row_max = jnp.max(scores[0], axis=1, keepdims=True)
            for s in range(1, topk):
                row_max = jnp.maximum(row_max, jnp.max(scores[s], axis=1, keepdims=True))
            row_sum = jnp.zeros((BLOCK, 1), jnp.float32)
            acc = jnp.zeros((BLOCK, HD), jnp.float32)
            for s in range(topk):
                e = jnp.exp(scores[s] - row_max)
                row_sum = row_sum + jnp.sum(e, axis=1, keepdims=True)
                acc = acc + jnp.dot(
                    e.astype(jnp.bfloat16), v_refs[s][:, cols],
                    preferred_element_type=jnp.float32,
                )
            att_ref[:, cols] = (acc / row_sum).astype(att_ref.dtype)


def project_kernel(a_ref, w_ref, o_ref):
    o_ref[0] = jnp.dot(a_ref[...], w_ref[...], preferred_element_type=jnp.float32).astype(
        o_ref.dtype
    )


def attend(meta, queries, kv_piece, topk):
    row_count, feat_width = queries.shape
    head_count = feat_width // HD

    def k_map(s):
        return lambda j, m: (m[s], 0)

    def v_map(s):
        return lambda j, m: (m[s], 1)

    blk = (BLOCK, feat_width)
    grid_spec = pltpu.PrefetchScalarGridSpec(
        num_scalar_prefetch=1,
        grid=(1,),
        in_specs=[pl.BlockSpec(blk, lambda j, m: (0, 0))]
        + [pl.BlockSpec(blk, k_map(s)) for s in range(topk)]
        + [pl.BlockSpec(blk, v_map(s)) for s in range(topk)],
        out_specs=pl.BlockSpec(blk, lambda j, m: (0, 0)),
    )
    return pl.pallas_call(
        functools.partial(attend_kernel, topk=topk, head_count=head_count),
        grid_spec=grid_spec,
        out_shape=jax.ShapeDtypeStruct((row_count, feat_width), queries.dtype),
        cost_estimate=pl.CostEstimate(
            flops=4 * head_count * BLOCK * topk * BLOCK * HD,
            transcendentals=head_count * BLOCK * topk * BLOCK,
            bytes_accessed=queries.size * 2 * (2 + 2 * topk),
        ),
    )(meta, queries, *([kv_piece] * (2 * topk)))


def project(att_full, w_group, halves):
    rows, inner = att_full.shape
    col_width = w_group.shape[1] // halves
    return pl.pallas_call(
        project_kernel,
        grid=(halves,),
        in_specs=[
            pl.BlockSpec((rows, inner), lambda k: (0, 0)),
            pl.BlockSpec((inner, col_width), lambda k: (0, k)),
        ],
        out_specs=pl.BlockSpec((1, rows, col_width), lambda k: (k, 0, 0)),
        out_shape=jax.ShapeDtypeStruct((halves, rows, col_width), att_full.dtype),
        cost_estimate=pl.CostEstimate(
            flops=2 * rows * inner * w_group.shape[1],
            transcendentals=0,
            bytes_accessed=att_full.size * 2 + w_group.size * 2 + rows * w_group.shape[1] * 2,
        ),
    )(att_full, w_group)


CTX = ("xl", "z", "core")
TP = ("y", "xh")


def per_device(queries, key_rows, value_rows, selection, out_weight):
    row_count, feat_width = queries.shape
    topk = selection.shape[1]
    y_size = lax.axis_size("y")
    xh_size = lax.axis_size("xh")
    y_place = lax.axis_index("y")
    ctx_place = lax.axis_index(CTX)
    own_choice = lax.dynamic_slice_in_dim(selection, ctx_place, 1, 0)[0]
    meta = jnp.concatenate([own_choice, ctx_place.astype(jnp.int32)[None]])
    kv_piece = lax.all_gather(
        jnp.concatenate([key_rows, value_rows], axis=1), CTX, axis=0, tiled=True
    )
    group_width = out_weight.shape[1] // y_size
    pieces = [lax.dynamic_slice_in_dim(out_weight, y_place * group_width, group_width, 1)]
    for shift in range(1, y_size):
        dest = (y_place + shift) % y_size
        sent = lax.dynamic_slice_in_dim(out_weight, dest * group_width, group_width, 1)
        pieces.append(lax.ppermute(sent, "y", [(i, (i + shift) % y_size) for i in range(y_size)]))
    by_shift = jnp.stack(pieces)
    order = (y_place - jnp.arange(y_size, dtype=jnp.int32)) % y_size
    w_group = jnp.take(by_shift, order, axis=0).reshape(y_size * out_weight.shape[0], group_width)
    kv_piece, w_group = lax.optimization_barrier((kv_piece, w_group))
    attended = attend(meta, queries, kv_piece, topk)
    att_full = lax.all_gather(attended, "y", axis=1, tiled=True)
    partial = project(att_full, w_group, xh_size)
    shares = lax.psum_scatter(partial, "xh", scatter_dimension=0, tiled=True)
    return shares.reshape(row_count, group_width // xh_size)


def solution(mesh):
    ctx_size, tp_size = mesh.devices.shape
    view = Mesh(
        mesh.devices.reshape(2, ctx_size // 4, 2, tp_size // 2, 2), ("xl", "z", "core", "y", "xh")
    )
    placed = (P(CTX, TP), P(CTX, TP), P(CTX, TP), P(), P(TP, None))
    return jax.shard_map(
        per_device, mesh=view, in_specs=placed, out_specs=P(CTX, TP), check_vma=False
    )
```

```python
import functools

import jax
import jax.numpy as jnp
from jax import lax
from jax.experimental import pallas as pl
from jax.experimental.pallas import tpu as pltpu
from jax.sharding import Mesh, PartitionSpec as P

HD = 128
BLOCK = 512

neg_fill = -1e30


def attend_kernel(meta_ref, q_ref, *refs, topk, head_count):
    k_refs = refs[:topk]
    v_refs = refs[topk : 2 * topk]
    att_ref = refs[2 * topk]
    if True:
        scaling = 1.0 / jnp.sqrt(jnp.float32(HD))
        q_block = meta_ref[topk]
        query_pos = q_block * BLOCK + lax.broadcasted_iota(jnp.int32, (BLOCK, BLOCK), 0)
        key_pos = meta_ref[0] * BLOCK + lax.broadcasted_iota(jnp.int32, (BLOCK, BLOCK), 1)
        causal = key_pos <= query_pos
        usable = [None] + [
            (meta_ref[s] != meta_ref[0]) & (meta_ref[s] < q_block) for s in range(1, topk)
        ]
        for h in range(head_count):
            cols = slice(h * HD, (h + 1) * HD)
            q = q_ref[:, cols]
            scores = []
            for s in range(topk):
                sc = lax.dot_general(
                    q, k_refs[s][:, cols], (((1,), (1,)), ((), ())),
                    preferred_element_type=jnp.float32,
                ) * scaling
                if s == 0:
                    sc = jnp.where(causal, sc, neg_fill)
                else:
                    sc = jnp.where(usable[s], sc, neg_fill)
                scores.append(sc)
            row_max = jnp.max(scores[0], axis=1, keepdims=True)
            for s in range(1, topk):
                row_max = jnp.maximum(row_max, jnp.max(scores[s], axis=1, keepdims=True))
            row_sum = jnp.zeros((BLOCK, 1), jnp.float32)
            acc = jnp.zeros((BLOCK, HD), jnp.float32)
            for s in range(topk):
                e = jnp.exp(scores[s] - row_max)
                row_sum = row_sum + jnp.sum(e, axis=1, keepdims=True)
                acc = acc + jnp.dot(
                    e.astype(jnp.bfloat16), v_refs[s][:, cols],
                    preferred_element_type=jnp.float32,
                )
            att_ref[:, cols] = (acc / row_sum).astype(att_ref.dtype)


def project_kernel(y_ref, *refs, shifts):
    a_refs = refs[:shifts]
    w_refs = refs[shifts : 2 * shifts]
    o_ref = refs[2 * shifts]
    acc = jnp.dot(a_refs[0][...], w_refs[0][...], preferred_element_type=jnp.float32)
    for sh in range(1, shifts):
        acc = acc + jnp.dot(a_refs[sh][...], w_refs[sh][...], preferred_element_type=jnp.float32)
    o_ref[0] = acc.astype(o_ref.dtype)


def attend(meta, queries, kv_piece, topk):
    row_count, feat_width = queries.shape
    head_count = feat_width // HD

    def k_map(s):
        return lambda j, m: (m[s], 0)

    def v_map(s):
        return lambda j, m: (m[s], 1)

    blk = (BLOCK, feat_width)
    grid_spec = pltpu.PrefetchScalarGridSpec(
        num_scalar_prefetch=1,
        grid=(1,),
        in_specs=[pl.BlockSpec(blk, lambda j, m: (0, 0))]
        + [pl.BlockSpec(blk, k_map(s)) for s in range(topk)]
        + [pl.BlockSpec(blk, v_map(s)) for s in range(topk)],
        out_specs=pl.BlockSpec(blk, lambda j, m: (0, 0)),
    )
    return pl.pallas_call(
        functools.partial(attend_kernel, topk=topk, head_count=head_count),
        grid_spec=grid_spec,
        out_shape=jax.ShapeDtypeStruct((row_count, feat_width), queries.dtype),
        cost_estimate=pl.CostEstimate(
            flops=4 * head_count * BLOCK * topk * BLOCK * HD,
            transcendentals=head_count * BLOCK * topk * BLOCK,
            bytes_accessed=queries.size * 2 * (2 + 2 * topk),
        ),
    )(meta, queries, *([kv_piece] * (2 * topk)))


def project(y_meta, att_full, out_weight, received, halves):
    rows = att_full.shape[0]
    shifts = len(received) + 1
    inner = att_full.shape[1] // shifts
    col_width = received[0].shape[1] // halves

    def a_map(sh):
        return lambda k, m: (0, (m[0] + shifts - sh) % shifts)

    grid_spec = pltpu.PrefetchScalarGridSpec(
        num_scalar_prefetch=1,
        grid=(halves,),
        in_specs=[pl.BlockSpec((rows, inner), a_map(sh)) for sh in range(shifts)]
        + [pl.BlockSpec((inner, col_width), lambda k, m: (0, m[0] * halves + k))]
        + [pl.BlockSpec((inner, col_width), lambda k, m: (0, k)) for _ in received],
        out_specs=pl.BlockSpec((1, rows, col_width), lambda k, m: (k, 0, 0)),
    )
    return pl.pallas_call(
        functools.partial(project_kernel, shifts=shifts),
        grid_spec=grid_spec,
        out_shape=jax.ShapeDtypeStruct((halves, rows, col_width), att_full.dtype),
        cost_estimate=pl.CostEstimate(
            flops=2 * rows * att_full.shape[1] * col_width * halves,
            transcendentals=0,
            bytes_accessed=att_full.size * 2 + shifts * inner * col_width * halves * 2
            + rows * col_width * halves * 2,
        ),
    )(y_meta, *([att_full] * shifts), out_weight, *received)


CTX = ("xl", "z", "core")
TP = ("y", "xh")


def per_device(queries, key_rows, value_rows, selection, out_weight):
    row_count, feat_width = queries.shape
    topk = selection.shape[1]
    y_size = lax.axis_size("y")
    xh_size = lax.axis_size("xh")
    y_place = lax.axis_index("y")
    ctx_place = lax.axis_index(CTX)
    own_choice = lax.dynamic_slice_in_dim(selection, ctx_place, 1, 0)[0]
    meta = jnp.concatenate([own_choice, ctx_place.astype(jnp.int32)[None]])
    kv_piece = lax.all_gather(
        jnp.concatenate([key_rows, value_rows], axis=1), CTX, axis=0, tiled=True
    )
    group_width = out_weight.shape[1] // y_size
    received = []
    for shift in range(1, y_size):
        dest = (y_place + shift) % y_size
        sent = lax.dynamic_slice_in_dim(out_weight, dest * group_width, group_width, 1)
        received.append(
            lax.ppermute(sent, "y", [(i, (i + shift) % y_size) for i in range(y_size)])
        )
    kv_piece, received = lax.optimization_barrier((kv_piece, received))
    attended = attend(meta, queries, kv_piece, topk)
    att_full = lax.all_gather(attended, "y", axis=1, tiled=True)
    y_meta = y_place.astype(jnp.int32)[None]
    partial = project(y_meta, att_full, out_weight, received, xh_size)
    shares = lax.psum_scatter(partial, "xh", scatter_dimension=0, tiled=True)
    return shares.reshape(row_count, group_width // xh_size)


def solution(mesh):
    ctx_size, tp_size = mesh.devices.shape
    view = Mesh(
        mesh.devices.reshape(2, ctx_size // 4, 2, tp_size // 2, 2), ("xl", "z", "core", "y", "xh")
    )
    placed = (P(CTX, TP), P(CTX, TP), P(CTX, TP), P(), P(TP, None))
    return jax.shard_map(
        per_device, mesh=view, in_specs=placed, out_specs=P(CTX, TP), check_vma=False
    )
```

```python
import functools

import jax
import jax.numpy as jnp
from jax import lax
from jax.experimental import pallas as pl
from jax.experimental.pallas import tpu as pltpu
from jax.sharding import Mesh, PartitionSpec as P

HD = 128
BLOCK = 512

neg_fill = -1e30


def attend_kernel(meta_ref, q_ref, *refs, topk, head_count):
    k_refs = refs[:topk]
    v_refs = refs[topk : 2 * topk]
    att_ref = refs[2 * topk]
    if True:
        scaling = 1.0 / jnp.sqrt(jnp.float32(HD))
        q_block = meta_ref[topk]
        query_pos = q_block * BLOCK + lax.broadcasted_iota(jnp.int32, (BLOCK, BLOCK), 0)
        key_pos = meta_ref[0] * BLOCK + lax.broadcasted_iota(jnp.int32, (BLOCK, BLOCK), 1)
        causal = key_pos <= query_pos
        usable = [None] + [
            (meta_ref[s] != meta_ref[0]) & (meta_ref[s] < q_block) for s in range(1, topk)
        ]
        for h in range(head_count):
            cols = slice(h * HD, (h + 1) * HD)
            q = q_ref[:, cols]
            scores = []
            for s in range(topk):
                sc = lax.dot_general(
                    q, k_refs[s][:, cols], (((1,), (1,)), ((), ())),
                    preferred_element_type=jnp.float32,
                ) * scaling
                if s == 0:
                    sc = jnp.where(causal, sc, neg_fill)
                else:
                    sc = jnp.where(usable[s], sc, neg_fill)
                scores.append(sc)
            row_max = jnp.max(scores[0], axis=1, keepdims=True)
            for s in range(1, topk):
                row_max = jnp.maximum(row_max, jnp.max(scores[s], axis=1, keepdims=True))
            row_sum = jnp.zeros((BLOCK, 1), jnp.float32)
            acc = jnp.zeros((BLOCK, HD), jnp.float32)
            for s in range(topk):
                e = jnp.exp(scores[s] - row_max)
                row_sum = row_sum + jnp.sum(e, axis=1, keepdims=True)
                acc = acc + jnp.dot(
                    e.astype(jnp.bfloat16), v_refs[s][:, cols],
                    preferred_element_type=jnp.float32,
                )
            att_ref[:, cols] = (acc / row_sum).astype(att_ref.dtype)


def project_kernel(y_ref, *refs, shifts):
    a_refs = refs[:shifts]
    w_refs = refs[shifts : 2 * shifts]
    o_ref = refs[2 * shifts]
    acc = jnp.dot(a_refs[0][...], w_refs[0][...], preferred_element_type=jnp.float32)
    for sh in range(1, shifts):
        acc = acc + jnp.dot(a_refs[sh][...], w_refs[sh][...], preferred_element_type=jnp.float32)
    o_ref[...] = acc.astype(o_ref.dtype)


def attend(meta, queries, kv_piece, topk):
    row_count, feat_width = queries.shape
    head_count = feat_width // HD

    def k_map(s):
        return lambda j, m: (m[s], 0)

    def v_map(s):
        return lambda j, m: (m[s], 1)

    blk = (BLOCK, feat_width)
    grid_spec = pltpu.PrefetchScalarGridSpec(
        num_scalar_prefetch=1,
        grid=(1,),
        in_specs=[pl.BlockSpec(blk, lambda j, m: (0, 0))]
        + [pl.BlockSpec(blk, k_map(s)) for s in range(topk)]
        + [pl.BlockSpec(blk, v_map(s)) for s in range(topk)],
        out_specs=pl.BlockSpec(blk, lambda j, m: (0, 0)),
    )
    return pl.pallas_call(
        functools.partial(attend_kernel, topk=topk, head_count=head_count),
        grid_spec=grid_spec,
        out_shape=jax.ShapeDtypeStruct((row_count, feat_width), queries.dtype),
        cost_estimate=pl.CostEstimate(
            flops=4 * head_count * BLOCK * topk * BLOCK * HD,
            transcendentals=head_count * BLOCK * topk * BLOCK,
            bytes_accessed=queries.size * 2 * (2 + 2 * topk),
        ),
    )(meta, queries, *([kv_piece] * (2 * topk)))


def project(meta, att_full, out_weight, received, halves, out_dtype):
    rows = att_full.shape[0]
    shifts = len(received) + 1
    inner = att_full.shape[1] // shifts
    col_width = received[0].shape[1] // halves

    def a_map(sh):
        return lambda i, m: (0, (m[0] + shifts - sh) % shifts)

    grid_spec = pltpu.PrefetchScalarGridSpec(
        num_scalar_prefetch=1,
        grid=(1,),
        in_specs=[pl.BlockSpec((rows, inner), a_map(sh)) for sh in range(shifts)]
        + [pl.BlockSpec((inner, col_width), lambda i, m: (0, m[0] * halves + m[1]))]
        + [pl.BlockSpec((inner, col_width), lambda i, m: (0, m[1])) for _ in received],
        out_specs=pl.BlockSpec((rows, col_width), lambda i, m: (0, 0)),
    )
    return pl.pallas_call(
        functools.partial(project_kernel, shifts=shifts),
        grid_spec=grid_spec,
        out_shape=jax.ShapeDtypeStruct((rows, col_width), out_dtype),
        cost_estimate=pl.CostEstimate(
            flops=2 * rows * att_full.shape[1] * col_width,
            transcendentals=0,
            bytes_accessed=att_full.size * 2 + shifts * inner * col_width * 2
            + rows * col_width * jnp.dtype(out_dtype).itemsize,
        ),
    )(meta, *([att_full] * shifts), out_weight, *received)


CTX = ("xl", "z", "core")
TP = ("y", "xh")


def per_device(queries, key_rows, value_rows, selection, out_weight):
    row_count, feat_width = queries.shape
    topk = selection.shape[1]
    y_size = lax.axis_size("y")
    xh_size = lax.axis_size("xh")
    y_place = lax.axis_index("y")
    ctx_place = lax.axis_index(CTX)
    own_choice = lax.dynamic_slice_in_dim(selection, ctx_place, 1, 0)[0]
    meta = jnp.concatenate([own_choice, ctx_place.astype(jnp.int32)[None]])
    kv_piece = lax.all_gather(
        jnp.concatenate([key_rows, value_rows], axis=1), CTX, axis=0, tiled=True
    )
    group_width = out_weight.shape[1] // y_size
    received = []
    for shift in range(1, y_size):
        dest = (y_place + shift) % y_size
        sent = lax.dynamic_slice_in_dim(out_weight, dest * group_width, group_width, 1)
        received.append(
            lax.ppermute(sent, "y", [(i, (i + shift) % y_size) for i in range(y_size)])
        )
    kv_piece, received = lax.optimization_barrier((kv_piece, received))
    attended = attend(meta, queries, kv_piece, topk)
    att_full = lax.all_gather(attended, "y", axis=1, tiled=True)
    xh_place = lax.axis_index("xh")
    other = jnp.stack([y_place, xh_size - 1 - xh_place]).astype(jnp.int32)
    mine = jnp.stack([y_place, xh_place]).astype(jnp.int32)
    sent = project(other, att_full, out_weight, received, xh_size, queries.dtype)
    got = lax.ppermute(sent, "xh", [(i, xh_size - 1 - i) for i in range(xh_size)])
    own = project(mine, att_full, out_weight, received, xh_size, jnp.float32)
    return (own + got.astype(jnp.float32)).astype(queries.dtype)


def solution(mesh):
    ctx_size, tp_size = mesh.devices.shape
    view = Mesh(
        mesh.devices.reshape(2, ctx_size // 4, 2, tp_size // 2, 2), ("xl", "z", "core", "y", "xh")
    )
    placed = (P(CTX, TP), P(CTX, TP), P(CTX, TP), P(), P(TP, None))
    return jax.shard_map(
        per_device, mesh=view, in_specs=placed, out_specs=P(CTX, TP), check_vma=False
    )
```

```python
import functools

import jax
import jax.numpy as jnp
from jax import lax
from jax.experimental import pallas as pl
from jax.experimental.pallas import tpu as pltpu
from jax.sharding import Mesh, PartitionSpec as P

HD = 128
BLOCK = 512

neg_fill = -1e30


def attend_kernel(meta_ref, q_ref, *refs, topk):
    k_refs = refs[:topk]
    v_refs = refs[topk : 2 * topk]
    att_ref = refs[2 * topk]
    scaling = 1.0 / jnp.sqrt(jnp.float32(HD))
    q_block = meta_ref[topk]
    query_pos = q_block * BLOCK + lax.broadcasted_iota(jnp.int32, (BLOCK, BLOCK), 0)
    key_pos = meta_ref[0] * BLOCK + lax.broadcasted_iota(jnp.int32, (BLOCK, BLOCK), 1)
    causal = key_pos <= query_pos
    q = q_ref[...]
    scores = []
    for s in range(topk):
        sc = lax.dot_general(
            q, k_refs[s][...], (((1,), (1,)), ((), ())), preferred_element_type=jnp.float32
        ) * scaling
        if s == 0:
            sc = jnp.where(causal, sc, neg_fill)
        else:
            usable = (meta_ref[s] != meta_ref[0]) & (meta_ref[s] < q_block)
            sc = jnp.where(usable, sc, neg_fill)
        scores.append(sc)
    row_max = jnp.max(scores[0], axis=1, keepdims=True)
    for s in range(1, topk):
        row_max = jnp.maximum(row_max, jnp.max(scores[s], axis=1, keepdims=True))
    row_sum = jnp.zeros((BLOCK, 1), jnp.float32)
    acc = jnp.zeros((BLOCK, HD), jnp.float32)
    for s in range(topk):
        e = jnp.exp(scores[s] - row_max)
        row_sum = row_sum + jnp.sum(e, axis=1, keepdims=True)
        acc = acc + jnp.dot(e.astype(jnp.bfloat16), v_refs[s][...], preferred_element_type=jnp.float32)
    att_ref[...] = (acc / row_sum).astype(att_ref.dtype)


def project_kernel(meta_ref, a_ref, w0_ref, w_ref, o_ref, acc_ref):
    sh = pl.program_id(0)

    @pl.when(sh == 0)
    def _():
        acc_ref[...] = jnp.dot(a_ref[...], w0_ref[...], preferred_element_type=jnp.float32)

    @pl.when(sh > 0)
    def _():
        acc_ref[...] += jnp.dot(a_ref[...], w_ref[0], preferred_element_type=jnp.float32)

    @pl.when(sh == pl.num_programs(0) - 1)
    def _():
        o_ref[...] = acc_ref[...].astype(o_ref.dtype)


def attend(meta, queries, kv_piece, topk):
    row_count, feat_width = queries.shape
    head_count = feat_width // HD

    def k_map(s):
        return lambda h, m: (m[s], h)

    def v_map(s):
        return lambda h, m: (m[s], head_count + h)

    blk = (BLOCK, HD)
    grid_spec = pltpu.PrefetchScalarGridSpec(
        num_scalar_prefetch=1,
        grid=(head_count,),
        in_specs=[pl.BlockSpec(blk, lambda h, m: (0, h))]
        + [pl.BlockSpec(blk, k_map(s)) for s in range(topk)]
        + [pl.BlockSpec(blk, v_map(s)) for s in range(topk)],
        out_specs=pl.BlockSpec(blk, lambda h, m: (0, h)),
    )
    return pl.pallas_call(
        functools.partial(attend_kernel, topk=topk),
        grid_spec=grid_spec,
        out_shape=jax.ShapeDtypeStruct((row_count, feat_width), queries.dtype),
        cost_estimate=pl.CostEstimate(
            flops=4 * head_count * BLOCK * topk * BLOCK * HD,
            transcendentals=head_count * BLOCK * topk * BLOCK,
            bytes_accessed=queries.size * 2 * (2 + 2 * topk),
        ),
    )(meta, queries, *([kv_piece] * (2 * topk)))


def project(meta, att_full, out_weight, received, halves, out_dtype):
    rows = att_full.shape[0]
    shifts = received.shape[0] + 1
    inner = att_full.shape[1] // shifts
    col_width = received.shape[2] // halves
    grid_spec = pltpu.PrefetchScalarGridSpec(
        num_scalar_prefetch=1,
        grid=(shifts,),
        in_specs=[
            pl.BlockSpec((rows, inner), lambda sh, m: (0, (m[0] + shifts - sh) % shifts)),
            pl.BlockSpec((inner, col_width), lambda sh, m: (0, m[0] * halves + m[1])),
            pl.BlockSpec(
                (1, inner, col_width), lambda sh, m: (jnp.maximum(sh - 1, 0), 0, m[1])
            ),
        ],
        out_specs=pl.BlockSpec((rows, col_width), lambda sh, m: (0, 0)),
        scratch_shapes=[pltpu.VMEM((rows, col_width), jnp.float32)],
    )
    return pl.pallas_call(
        project_kernel,
        grid_spec=grid_spec,
        out_shape=jax.ShapeDtypeStruct((rows, col_width), out_dtype),
        compiler_params=pltpu.CompilerParams(dimension_semantics=("arbitrary",)),
        cost_estimate=pl.CostEstimate(
            flops=2 * rows * att_full.shape[1] * col_width,
            transcendentals=0,
            bytes_accessed=att_full.size * 2 + shifts * inner * col_width * 2
            + rows * col_width * jnp.dtype(out_dtype).itemsize,
        ),
    )(meta, att_full, out_weight, received)


CTX = ("xl", "z", "core")
TP = ("y", "xh")


def per_device(queries, key_rows, value_rows, selection, out_weight):
    row_count, feat_width = queries.shape
    topk = selection.shape[1]
    y_size = lax.axis_size("y")
    xh_size = lax.axis_size("xh")
    y_place = lax.axis_index("y")
    ctx_place = lax.axis_index(CTX)
    own_choice = lax.dynamic_slice_in_dim(selection, ctx_place, 1, 0)[0]
    meta = jnp.concatenate([own_choice, ctx_place.astype(jnp.int32)[None]])
    kv_piece = lax.all_gather(
        jnp.concatenate([key_rows, value_rows], axis=1), CTX, axis=0, tiled=True
    )
    group_width = out_weight.shape[1] // y_size
    received = []
    for shift in range(1, y_size):
        dest = (y_place + shift) % y_size
        sent = lax.dynamic_slice_in_dim(out_weight, dest * group_width, group_width, 1)
        received.append(
            lax.ppermute(sent, "y", [(i, (i + shift) % y_size) for i in range(y_size)])
        )
    kv_piece, received = lax.optimization_barrier((kv_piece, jnp.stack(received)))
    attended = attend(meta, queries, kv_piece, topk)
    att_full = lax.all_gather(attended, "y", axis=1, tiled=True)
    xh_place = lax.axis_index("xh")
    other = jnp.stack([y_place, xh_size - 1 - xh_place]).astype(jnp.int32)
    mine = jnp.stack([y_place, xh_place]).astype(jnp.int32)
    sent = project(other, att_full, out_weight, received, xh_size, queries.dtype)
    got = lax.ppermute(sent, "xh", [(i, xh_size - 1 - i) for i in range(xh_size)])
    own = project(mine, att_full, out_weight, received, xh_size, jnp.float32)
    return (own + got.astype(jnp.float32)).astype(queries.dtype)


def solution(mesh):
    ctx_size, tp_size = mesh.devices.shape
    view = Mesh(
        mesh.devices.reshape(2, ctx_size // 4, 2, tp_size // 2, 2), ("xl", "z", "core", "y", "xh")
    )
    placed = (P(CTX, TP), P(CTX, TP), P(CTX, TP), P(), P(TP, None))
    return jax.shard_map(
        per_device, mesh=view, in_specs=placed, out_specs=P(CTX, TP), check_vma=False
    )
```

```python
import functools

import jax
import jax.numpy as jnp
from jax import lax
from jax.experimental import pallas as pl
from jax.experimental.pallas import tpu as pltpu
from jax.sharding import Mesh, PartitionSpec as P

HD = 128
BLOCK = 512

neg_fill = -1e30


def attend_kernel(meta_ref, q_ref, *refs, topk, head_count):
    k_refs = refs[:topk]
    v_refs = refs[topk : 2 * topk]
    att_ref = refs[2 * topk]
    if True:
        scaling = 1.0 / jnp.sqrt(jnp.float32(HD))
        q_block = meta_ref[topk]
        query_pos = q_block * BLOCK + lax.broadcasted_iota(jnp.int32, (BLOCK, BLOCK), 0)
        key_pos = meta_ref[0] * BLOCK + lax.broadcasted_iota(jnp.int32, (BLOCK, BLOCK), 1)
        causal = key_pos <= query_pos
        usable = [None] + [
            (meta_ref[s] != meta_ref[0]) & (meta_ref[s] < q_block) for s in range(1, topk)
        ]
        for h in range(head_count):
            cols = slice(h * HD, (h + 1) * HD)
            q = q_ref[:, cols]
            scores = []
            for s in range(topk):
                sc = lax.dot_general(
                    q, k_refs[s][:, cols], (((1,), (1,)), ((), ())),
                    preferred_element_type=jnp.float32,
                ) * scaling
                if s == 0:
                    sc = jnp.where(causal, sc, neg_fill)
                else:
                    sc = jnp.where(usable[s], sc, neg_fill)
                scores.append(sc)
            row_max = jnp.max(scores[0], axis=1, keepdims=True)
            for s in range(1, topk):
                row_max = jnp.maximum(row_max, jnp.max(scores[s], axis=1, keepdims=True))
            row_sum = jnp.zeros((BLOCK, 1), jnp.float32)
            acc = jnp.zeros((BLOCK, HD), jnp.float32)
            for s in range(topk):
                e = jnp.exp(scores[s] - row_max)
                row_sum = row_sum + jnp.sum(e, axis=1, keepdims=True)
                acc = acc + jnp.dot(
                    e.astype(jnp.bfloat16), v_refs[s][:, cols],
                    preferred_element_type=jnp.float32,
                )
            att_ref[:, cols] = (acc / row_sum).astype(att_ref.dtype)


def project_kernel(y_ref, *refs, shifts):
    a_refs = refs[:shifts]
    w_refs = refs[shifts : 2 * shifts]
    o_ref = refs[2 * shifts]
    acc = jnp.dot(a_refs[0][...], w_refs[0][...], preferred_element_type=jnp.float32)
    for sh in range(1, shifts):
        acc = acc + jnp.dot(a_refs[sh][...], w_refs[sh][...], preferred_element_type=jnp.float32)
    o_ref[...] = acc.astype(o_ref.dtype)


def attend(meta, queries, kv_piece, topk):
    row_count, feat_width = queries.shape
    head_count = feat_width // HD

    def k_map(s):
        return lambda j, m: (m[s], 0)

    def v_map(s):
        return lambda j, m: (m[s], 1)

    blk = (BLOCK, feat_width)
    grid_spec = pltpu.PrefetchScalarGridSpec(
        num_scalar_prefetch=1,
        grid=(1,),
        in_specs=[pl.BlockSpec(blk, lambda j, m: (0, 0))]
        + [pl.BlockSpec(blk, k_map(s)) for s in range(topk)]
        + [pl.BlockSpec(blk, v_map(s)) for s in range(topk)],
        out_specs=pl.BlockSpec(blk, lambda j, m: (0, 0)),
    )
    return pl.pallas_call(
        functools.partial(attend_kernel, topk=topk, head_count=head_count),
        grid_spec=grid_spec,
        out_shape=jax.ShapeDtypeStruct((row_count, feat_width), queries.dtype),
        cost_estimate=pl.CostEstimate(
            flops=4 * head_count * BLOCK * topk * BLOCK * HD,
            transcendentals=head_count * BLOCK * topk * BLOCK,
            bytes_accessed=queries.size * 2 * (2 + 2 * topk),
        ),
    )(meta, queries, *([kv_piece] * (2 * topk)))


def project(meta, pieces, out_weight, received, halves, out_dtype):
    rows, inner = pieces[0].shape
    shifts = len(received) + 1
    col_width = received[0].shape[1] // halves
    grid_spec = pltpu.PrefetchScalarGridSpec(
        num_scalar_prefetch=1,
        grid=(1,),
        in_specs=[pl.BlockSpec((rows, inner), lambda i, m: (0, 0)) for _ in range(shifts)]
        + [pl.BlockSpec((inner, col_width), lambda i, m: (0, m[0] * halves + m[1]))]
        + [pl.BlockSpec((inner, col_width), lambda i, m: (0, m[1])) for _ in received],
        out_specs=pl.BlockSpec((rows, col_width), lambda i, m: (0, 0)),
    )
    return pl.pallas_call(
        functools.partial(project_kernel, shifts=shifts),
        grid_spec=grid_spec,
        out_shape=jax.ShapeDtypeStruct((rows, col_width), out_dtype),
        cost_estimate=pl.CostEstimate(
            flops=2 * rows * inner * shifts * col_width,
            transcendentals=0,
            bytes_accessed=rows * inner * shifts * 2 + shifts * inner * col_width * 2
            + rows * col_width * jnp.dtype(out_dtype).itemsize,
        ),
    )(meta, *pieces, out_weight, *received)


CTX = ("xl", "z", "core")
TP = ("y", "xh")


def per_device(queries, key_rows, value_rows, selection, out_weight):
    row_count, feat_width = queries.shape
    topk = selection.shape[1]
    y_size = lax.axis_size("y")
    xh_size = lax.axis_size("xh")
    y_place = lax.axis_index("y")
    ctx_place = lax.axis_index(CTX)
    own_choice = lax.dynamic_slice_in_dim(selection, ctx_place, 1, 0)[0]
    meta = jnp.concatenate([own_choice, ctx_place.astype(jnp.int32)[None]])
    kv_piece = lax.all_gather(
        jnp.concatenate([key_rows, value_rows], axis=1), CTX, axis=0, tiled=True
    )
    group_width = out_weight.shape[1] // y_size
    received = []
    for shift in range(1, y_size):
        dest = (y_place + shift) % y_size
        sent = lax.dynamic_slice_in_dim(out_weight, dest * group_width, group_width, 1)
        received.append(
            lax.ppermute(sent, "y", [(i, (i + shift) % y_size) for i in range(y_size)])
        )
    kv_piece, received = lax.optimization_barrier((kv_piece, received))
    attended = attend(meta, queries, kv_piece, topk)
    pieces = [attended] + [
        lax.ppermute(attended, "y", [(i, (i + shift) % y_size) for i in range(y_size)])
        for shift in range(1, y_size)
    ]
    xh_place = lax.axis_index("xh")
    other = jnp.stack([y_place, xh_size - 1 - xh_place]).astype(jnp.int32)
    mine = jnp.stack([y_place, xh_place]).astype(jnp.int32)
    sent = project(other, pieces, out_weight, received, xh_size, queries.dtype)
    got = lax.ppermute(sent, "xh", [(i, xh_size - 1 - i) for i in range(xh_size)])
    own = project(mine, pieces, out_weight, received, xh_size, jnp.float32)
    return (own + got.astype(jnp.float32)).astype(queries.dtype)


def solution(mesh):
    ctx_size, tp_size = mesh.devices.shape
    view = Mesh(
        mesh.devices.reshape(2, ctx_size // 4, 2, tp_size // 2, 2), ("xl", "z", "core", "y", "xh")
    )
    placed = (P(CTX, TP), P(CTX, TP), P(CTX, TP), P(), P(TP, None))
    return jax.shard_map(
        per_device, mesh=view, in_specs=placed, out_specs=P(CTX, TP), check_vma=False
    )
```

```python
import functools

import jax
import jax.numpy as jnp
from jax import lax
from jax.experimental import pallas as pl
from jax.experimental.pallas import tpu as pltpu
from jax.sharding import Mesh, PartitionSpec as P

HD = 128
BLOCK = 512

neg_fill = -1e30


def own_kernel(meta_ref, q_ref, k_ref, v_ref, acc_ref, max_ref, sum_ref, *, head_count):
    scaling = 1.0 / jnp.sqrt(jnp.float32(HD))
    query_pos = meta_ref[0] * BLOCK + lax.broadcasted_iota(jnp.int32, (BLOCK, BLOCK), 0)
    key_pos = meta_ref[1] * BLOCK + lax.broadcasted_iota(jnp.int32, (BLOCK, BLOCK), 1)
    causal = key_pos <= query_pos
    for h in range(head_count):
        cols = slice(h * HD, (h + 1) * HD)
        sc = lax.dot_general(
            q_ref[:, cols], k_ref[:, cols], (((1,), (1,)), ((), ())),
            preferred_element_type=jnp.float32,
        ) * scaling
        sc = jnp.where(causal, sc, neg_fill)
        row_max = jnp.max(sc, axis=1, keepdims=True)
        e = jnp.exp(sc - row_max)
        max_ref[h] = row_max
        sum_ref[h] = jnp.sum(e, axis=1, keepdims=True)
        acc_ref[:, cols] = jnp.dot(
            e.astype(jnp.bfloat16), v_ref[:, cols], preferred_element_type=jnp.float32
        )


def attend_kernel(meta_ref, q_ref, *refs, topk, head_count):
    k_refs = refs[: topk - 1]
    v_refs = refs[topk - 1 : 2 * topk - 2]
    acc0_ref, max0_ref, sum0_ref, att_ref = refs[2 * topk - 2 :]
    scaling = 1.0 / jnp.sqrt(jnp.float32(HD))
    q_block = meta_ref[topk]
    usable = [(meta_ref[s] != meta_ref[0]) & (meta_ref[s] < q_block) for s in range(1, topk)]
    for h in range(head_count):
        cols = slice(h * HD, (h + 1) * HD)
        q = q_ref[:, cols]
        scores = []
        for s in range(topk - 1):
            sc = lax.dot_general(
                q, k_refs[s][:, cols], (((1,), (1,)), ((), ())),
                preferred_element_type=jnp.float32,
            ) * scaling
            scores.append(jnp.where(usable[s], sc, neg_fill))
        max0 = max0_ref[h]
        row_max = max0
        for sc in scores:
            row_max = jnp.maximum(row_max, jnp.max(sc, axis=1, keepdims=True))
        rescale = jnp.exp(max0 - row_max)
        row_sum = sum0_ref[h] * rescale
        acc = acc0_ref[:, cols] * rescale
        for s in range(topk - 1):
            e = jnp.exp(scores[s] - row_max)
            row_sum = row_sum + jnp.sum(e, axis=1, keepdims=True)
            acc = acc + jnp.dot(
                e.astype(jnp.bfloat16), v_refs[s][:, cols], preferred_element_type=jnp.float32
            )
        att_ref[:, cols] = (acc / row_sum).astype(att_ref.dtype)


def project_kernel(y_ref, *refs, shifts):
    a_refs = refs[:shifts]
    w_refs = refs[shifts : 2 * shifts]
    o_ref = refs[2 * shifts]
    acc = jnp.dot(a_refs[0][...], w_refs[0][...], preferred_element_type=jnp.float32)
    for sh in range(1, shifts):
        acc = acc + jnp.dot(a_refs[sh][...], w_refs[sh][...], preferred_element_type=jnp.float32)
    o_ref[...] = acc.astype(o_ref.dtype)


def attend_own(meta, queries, key_rows, value_rows):
    row_count, feat_width = queries.shape
    head_count = feat_width // HD
    full = pl.BlockSpec((row_count, feat_width), lambda j, m: (0, 0))
    grid_spec = pltpu.PrefetchScalarGridSpec(
        num_scalar_prefetch=1,
        grid=(1,),
        in_specs=[full, full, full],
        out_specs=[
            full,
            pl.BlockSpec((head_count, row_count, 1), lambda j, m: (0, 0, 0)),
            pl.BlockSpec((head_count, row_count, 1), lambda j, m: (0, 0, 0)),
        ],
    )
    return pl.pallas_call(
        functools.partial(own_kernel, head_count=head_count),
        grid_spec=grid_spec,
        out_shape=[
            jax.ShapeDtypeStruct((row_count, feat_width), jnp.float32),
            jax.ShapeDtypeStruct((head_count, row_count, 1), jnp.float32),
            jax.ShapeDtypeStruct((head_count, row_count, 1), jnp.float32),
        ],
        cost_estimate=pl.CostEstimate(
            flops=4 * head_count * BLOCK * BLOCK * HD,
            transcendentals=head_count * BLOCK * BLOCK,
            bytes_accessed=queries.size * 2 * 3 + queries.size * 4,
        ),
    )(meta, queries, key_rows, value_rows)


def attend(meta, queries, kv_piece, own_part, topk):
    row_count, feat_width = queries.shape
    head_count = feat_width // HD

    def k_map(s):
        return lambda j, m: (m[s], 0)

    def v_map(s):
        return lambda j, m: (m[s], 1)

    blk = (BLOCK, feat_width)
    stat = pl.BlockSpec((head_count, row_count, 1), lambda j, m: (0, 0, 0))
    grid_spec = pltpu.PrefetchScalarGridSpec(
        num_scalar_prefetch=1,
        grid=(1,),
        in_specs=[pl.BlockSpec(blk, lambda j, m: (0, 0))]
        + [pl.BlockSpec(blk, k_map(s)) for s in range(1, topk)]
        + [pl.BlockSpec(blk, v_map(s)) for s in range(1, topk)]
        + [pl.BlockSpec(blk, lambda j, m: (0, 0)), stat, stat],
        out_specs=pl.BlockSpec(blk, lambda j, m: (0, 0)),
    )
    return pl.pallas_call(
        functools.partial(attend_kernel, topk=topk, head_count=head_count),
        grid_spec=grid_spec,
        out_shape=jax.ShapeDtypeStruct((row_count, feat_width), queries.dtype),
        cost_estimate=pl.CostEstimate(
            flops=4 * head_count * BLOCK * (topk - 1) * BLOCK * HD,
            transcendentals=head_count * BLOCK * (topk - 1) * BLOCK,
            bytes_accessed=queries.size * 2 * (2 + 2 * topk) + queries.size * 4,
        ),
    )(meta, queries, *([kv_piece] * (2 * topk - 2)), *own_part)


def project(meta, pieces, out_weight, received, halves, out_dtype):
    rows, inner = pieces[0].shape
    shifts = len(received) + 1
    col_width = received[0].shape[1] // halves
    grid_spec = pltpu.PrefetchScalarGridSpec(
        num_scalar_prefetch=1,
        grid=(1,),
        in_specs=[pl.BlockSpec((rows, inner), lambda i, m: (0, 0)) for _ in range(shifts)]
        + [pl.BlockSpec((inner, col_width), lambda i, m: (0, m[0] * halves + m[1]))]
        + [pl.BlockSpec((inner, col_width), lambda i, m: (0, m[1])) for _ in received],
        out_specs=pl.BlockSpec((rows, col_width), lambda i, m: (0, 0)),
    )
    return pl.pallas_call(
        functools.partial(project_kernel, shifts=shifts),
        grid_spec=grid_spec,
        out_shape=jax.ShapeDtypeStruct((rows, col_width), out_dtype),
        cost_estimate=pl.CostEstimate(
            flops=2 * rows * inner * shifts * col_width,
            transcendentals=0,
            bytes_accessed=rows * inner * shifts * 2 + shifts * inner * col_width * 2
            + rows * col_width * jnp.dtype(out_dtype).itemsize,
        ),
    )(meta, *pieces, out_weight, *received)


CTX = ("xl", "z", "core")
TP = ("y", "xh")


def per_device(queries, key_rows, value_rows, selection, out_weight):
    row_count, feat_width = queries.shape
    topk = selection.shape[1]
    y_size = lax.axis_size("y")
    xh_size = lax.axis_size("xh")
    y_place = lax.axis_index("y")
    ctx_place = lax.axis_index(CTX)
    own_choice = lax.dynamic_slice_in_dim(selection, ctx_place, 1, 0)[0]
    meta = jnp.concatenate([own_choice, ctx_place.astype(jnp.int32)[None]])
    kv_piece = lax.all_gather(
        jnp.concatenate([key_rows, value_rows], axis=1), CTX, axis=0, tiled=True
    )
    group_width = out_weight.shape[1] // y_size
    received = []
    for shift in range(1, y_size):
        dest = (y_place + shift) % y_size
        sent = lax.dynamic_slice_in_dim(out_weight, dest * group_width, group_width, 1)
        received.append(
            lax.ppermute(sent, "y", [(i, (i + shift) % y_size) for i in range(y_size)])
        )
    own_part = attend_own(meta[topk:topk + 1].repeat(2), queries, key_rows, value_rows)
    kv_piece, received, own_part = lax.optimization_barrier((kv_piece, received, own_part))
    attended = attend(meta, queries, kv_piece, own_part, topk)
    pieces = [attended] + [
        lax.ppermute(attended, "y", [(i, (i + shift) % y_size) for i in range(y_size)])
        for shift in range(1, y_size)
    ]
    xh_place = lax.axis_index("xh")
    other = jnp.stack([y_place, xh_size - 1 - xh_place]).astype(jnp.int32)
    mine = jnp.stack([y_place, xh_place]).astype(jnp.int32)
    sent = project(other, pieces, out_weight, received, xh_size, queries.dtype)
    got = lax.ppermute(sent, "xh", [(i, xh_size - 1 - i) for i in range(xh_size)])
    own = project(mine, pieces, out_weight, received, xh_size, jnp.float32)
    return (own + got.astype(jnp.float32)).astype(queries.dtype)


def solution(mesh):
    ctx_size, tp_size = mesh.devices.shape
    view = Mesh(
        mesh.devices.reshape(2, ctx_size // 4, 2, tp_size // 2, 2), ("xl", "z", "core", "y", "xh")
    )
    placed = (P(CTX, TP), P(CTX, TP), P(CTX, TP), P(), P(TP, None))
    return jax.shard_map(
        per_device, mesh=view, in_specs=placed, out_specs=P(CTX, TP), check_vma=False
    )
```

```python
import functools

import jax
import jax.numpy as jnp
from jax import lax
from jax.experimental import pallas as pl
from jax.experimental.pallas import tpu as pltpu
from jax.sharding import Mesh, PartitionSpec as P

HD = 128
BLOCK = 512

neg_fill = -1e30


def attend_kernel(meta_ref, q_ref, *refs, topk, head_count):
    k_refs = refs[:topk]
    v_refs = refs[topk : 2 * topk]
    att_ref = refs[2 * topk]
    if True:
        scaling = 1.0 / jnp.sqrt(jnp.float32(HD))
        q_block = meta_ref[topk]
        query_pos = q_block * BLOCK + lax.broadcasted_iota(jnp.int32, (BLOCK, BLOCK), 0)
        key_pos = meta_ref[0] * BLOCK + lax.broadcasted_iota(jnp.int32, (BLOCK, BLOCK), 1)
        causal = key_pos <= query_pos
        usable = [None] + [
            (meta_ref[s] != meta_ref[0]) & (meta_ref[s] < q_block) for s in range(1, topk)
        ]
        for h in range(head_count):
            cols = slice(h * HD, (h + 1) * HD)
            q = q_ref[:, cols]
            scores = []
            for s in range(topk):
                sc = lax.dot_general(
                    q, k_refs[s][:, cols], (((1,), (1,)), ((), ())),
                    preferred_element_type=jnp.float32,
                ) * scaling
                if s == 0:
                    sc = jnp.where(causal, sc, neg_fill)
                else:
                    sc = jnp.where(usable[s], sc, neg_fill)
                scores.append(sc)
            row_max = jnp.max(scores[0], axis=1, keepdims=True)
            for s in range(1, topk):
                row_max = jnp.maximum(row_max, jnp.max(scores[s], axis=1, keepdims=True))
            row_sum = jnp.zeros((BLOCK, 1), jnp.float32)
            acc = jnp.zeros((BLOCK, HD), jnp.float32)
            for s in range(topk):
                e = jnp.exp(scores[s] - row_max)
                row_sum = row_sum + jnp.sum(e, axis=1, keepdims=True)
                acc = acc + jnp.dot(
                    e.astype(jnp.bfloat16), v_refs[s][:, cols],
                    preferred_element_type=jnp.float32,
                )
            att_ref[:, cols] = (acc / row_sum).astype(att_ref.dtype)


def project_kernel(y_ref, *refs, shifts):
    a_refs = refs[:shifts]
    w_refs = refs[shifts : 2 * shifts]
    o_ref = refs[2 * shifts]
    acc = jnp.dot(a_refs[0][...], w_refs[0][...], preferred_element_type=jnp.float32)
    for sh in range(1, shifts):
        acc = acc + jnp.dot(a_refs[sh][...], w_refs[sh][...], preferred_element_type=jnp.float32)
    o_ref[...] = acc.astype(o_ref.dtype)


def attend(meta, queries, kv_piece, topk):
    row_count, feat_width = queries.shape
    head_count = feat_width // HD

    def k_map(s):
        return lambda j, m: (m[s], 0)

    def v_map(s):
        return lambda j, m: (m[s], 1)

    blk = (BLOCK, feat_width)
    grid_spec = pltpu.PrefetchScalarGridSpec(
        num_scalar_prefetch=1,
        grid=(1,),
        in_specs=[pl.BlockSpec(blk, lambda j, m: (0, 0))]
        + [pl.BlockSpec(blk, k_map(s)) for s in range(topk)]
        + [pl.BlockSpec(blk, v_map(s)) for s in range(topk)],
        out_specs=pl.BlockSpec(blk, lambda j, m: (0, 0)),
    )
    return pl.pallas_call(
        functools.partial(attend_kernel, topk=topk, head_count=head_count),
        grid_spec=grid_spec,
        out_shape=jax.ShapeDtypeStruct((row_count, feat_width), queries.dtype),
        cost_estimate=pl.CostEstimate(
            flops=4 * head_count * BLOCK * topk * BLOCK * HD,
            transcendentals=head_count * BLOCK * topk * BLOCK,
            bytes_accessed=queries.size * 2 * (2 + 2 * topk),
        ),
    )(meta, queries, *([kv_piece] * (2 * topk)))


def project(meta, pieces, out_weight, received, halves, out_dtype):
    rows, inner = pieces[0].shape
    shifts = len(received) + 1
    col_width = received[0].shape[1] // halves
    grid_spec = pltpu.PrefetchScalarGridSpec(
        num_scalar_prefetch=1,
        grid=(1,),
        in_specs=[pl.BlockSpec((rows, inner), lambda i, m: (0, 0)) for _ in range(shifts)]
        + [pl.BlockSpec((inner, col_width), lambda i, m: (0, m[0] * halves + m[1]))]
        + [pl.BlockSpec((inner, col_width), lambda i, m: (0, m[1])) for _ in received],
        out_specs=pl.BlockSpec((rows, col_width), lambda i, m: (0, 0)),
    )
    return pl.pallas_call(
        functools.partial(project_kernel, shifts=shifts),
        grid_spec=grid_spec,
        out_shape=jax.ShapeDtypeStruct((rows, col_width), out_dtype),
        cost_estimate=pl.CostEstimate(
            flops=2 * rows * inner * shifts * col_width,
            transcendentals=0,
            bytes_accessed=rows * inner * shifts * 2 + shifts * inner * col_width * 2
            + rows * col_width * jnp.dtype(out_dtype).itemsize,
        ),
    )(meta, *pieces, out_weight, *received)


CTX = ("xl", "z", "core")
TP = ("y", "xh")


def per_device(queries, key_rows, value_rows, selection, out_weight):
    row_count, feat_width = queries.shape
    topk = selection.shape[1]
    y_size = lax.axis_size("y")
    xh_size = lax.axis_size("xh")
    y_place = lax.axis_index("y")
    ctx_place = lax.axis_index(CTX)
    own_choice = lax.dynamic_slice_in_dim(selection, ctx_place, 1, 0)[0]
    meta = jnp.concatenate([own_choice, ctx_place.astype(jnp.int32)[None]])
    kv_piece = lax.all_gather(
        jnp.concatenate([key_rows, value_rows], axis=1), CTX, axis=0, tiled=True
    )
    group_width = out_weight.shape[1] // y_size
    received = []
    for shift in range(1, y_size):
        dest = (y_place + shift) % y_size
        sent = lax.dynamic_slice_in_dim(out_weight, dest * group_width, group_width, 1)
        received.append(
            lax.ppermute(sent, "y", [(i, (i + shift) % y_size) for i in range(y_size)])
        )
    kv_piece, received = lax.optimization_barrier((kv_piece, received))
    attended = attend(meta, queries, kv_piece, topk)
    pieces = [attended] + [
        lax.ppermute(attended, "y", [(i, (i + shift) % y_size) for i in range(y_size)])
        for shift in range(1, y_size)
    ]
    xh_place = lax.axis_index("xh")
    other = jnp.stack([y_place, xh_size - 1 - xh_place]).astype(jnp.int32)
    mine = jnp.stack([y_place, xh_place]).astype(jnp.int32)
    sent = project(other, pieces, out_weight, received, xh_size, queries.dtype)
    swap = [(i, xh_size - 1 - i) for i in range(xh_size)]
    split = row_count // 2
    got = [lax.ppermute(sent[:split], "xh", swap), lax.ppermute(sent[split:], "xh", swap)]
    own = project(mine, pieces, out_weight, received, xh_size, jnp.float32)
    return (own + jnp.concatenate(got).astype(jnp.float32)).astype(queries.dtype)


def solution(mesh):
    ctx_size, tp_size = mesh.devices.shape
    view = Mesh(
        mesh.devices.reshape(2, ctx_size // 4, 2, tp_size // 2, 2), ("xl", "z", "core", "y", "xh")
    )
    placed = (P(CTX, TP), P(CTX, TP), P(CTX, TP), P(), P(TP, None))
    return jax.shard_map(
        per_device, mesh=view, in_specs=placed, out_specs=P(CTX, TP), check_vma=False
    )
```

```python
import functools

import jax
import jax.numpy as jnp
from jax import lax
from jax.experimental import pallas as pl
from jax.experimental.pallas import tpu as pltpu
from jax.sharding import Mesh, PartitionSpec as P

HD = 128
BLOCK = 512

neg_fill = -1e30


def attend_kernel(meta_ref, q_ref, *refs, topk, head_count):
    k_refs = refs[:topk]
    v_refs = refs[topk : 2 * topk]
    att_ref = refs[2 * topk]
    if True:
        scaling = 1.0 / jnp.sqrt(jnp.float32(HD))
        q_block = meta_ref[topk]
        query_pos = q_block * BLOCK + lax.broadcasted_iota(jnp.int32, (BLOCK, BLOCK), 0)
        key_pos = meta_ref[0] * BLOCK + lax.broadcasted_iota(jnp.int32, (BLOCK, BLOCK), 1)
        causal = key_pos <= query_pos
        usable = [None] + [
            (meta_ref[s] != meta_ref[0]) & (meta_ref[s] < q_block) for s in range(1, topk)
        ]
        for h in range(head_count):
            cols = slice(h * HD, (h + 1) * HD)
            q = q_ref[:, cols]
            scores = []
            for s in range(topk):
                sc = lax.dot_general(
                    q, k_refs[s][:, cols], (((1,), (1,)), ((), ())),
                    preferred_element_type=jnp.float32,
                ) * scaling
                if s == 0:
                    sc = jnp.where(causal, sc, neg_fill)
                else:
                    sc = jnp.where(usable[s], sc, neg_fill)
                scores.append(sc)
            row_max = jnp.max(scores[0], axis=1, keepdims=True)
            for s in range(1, topk):
                row_max = jnp.maximum(row_max, jnp.max(scores[s], axis=1, keepdims=True))
            row_sum = jnp.zeros((BLOCK, 1), jnp.float32)
            acc = jnp.zeros((BLOCK, HD), jnp.float32)
            for s in range(topk):
                e = jnp.exp(scores[s] - row_max)
                row_sum = row_sum + jnp.sum(e, axis=1, keepdims=True)
                acc = acc + jnp.dot(
                    e.astype(jnp.bfloat16), v_refs[s][:, cols],
                    preferred_element_type=jnp.float32,
                )
            att_ref[:, cols] = (acc / row_sum).astype(att_ref.dtype)


def project_kernel(y_ref, *refs, shifts):
    a_refs = refs[:shifts]
    w_refs = refs[shifts : 2 * shifts]
    o_ref = refs[2 * shifts]
    acc = jnp.dot(a_refs[0][...], w_refs[0][...], preferred_element_type=jnp.float32)
    for sh in range(1, shifts):
        acc = acc + jnp.dot(a_refs[sh][...], w_refs[sh][...], preferred_element_type=jnp.float32)
    o_ref[...] = acc.astype(o_ref.dtype)


def attend(meta, queries, kv_piece, topk):
    row_count, feat_width = queries.shape
    head_count = feat_width // HD

    def k_map(s):
        return lambda j, m: (m[s], 0)

    def v_map(s):
        return lambda j, m: (m[s], 1)

    blk = (BLOCK, feat_width)
    grid_spec = pltpu.PrefetchScalarGridSpec(
        num_scalar_prefetch=1,
        grid=(1,),
        in_specs=[pl.BlockSpec(blk, lambda j, m: (0, 0))]
        + [pl.BlockSpec(blk, k_map(s)) for s in range(topk)]
        + [pl.BlockSpec(blk, v_map(s)) for s in range(topk)],
        out_specs=pl.BlockSpec(blk, lambda j, m: (0, 0)),
    )
    return pl.pallas_call(
        functools.partial(attend_kernel, topk=topk, head_count=head_count),
        grid_spec=grid_spec,
        out_shape=jax.ShapeDtypeStruct((row_count, feat_width), queries.dtype),
        cost_estimate=pl.CostEstimate(
            flops=4 * head_count * BLOCK * topk * BLOCK * HD,
            transcendentals=head_count * BLOCK * topk * BLOCK,
            bytes_accessed=queries.size * 2 * (2 + 2 * topk),
        ),
    )(meta, queries, *([kv_piece] * (2 * topk)))


def project(meta, pieces, out_weight, received, halves, out_dtype):
    rows, inner = pieces[0].shape
    shifts = len(received) + 1
    col_width = received[0].shape[1] // halves
    grid_spec = pltpu.PrefetchScalarGridSpec(
        num_scalar_prefetch=1,
        grid=(1,),
        in_specs=[pl.BlockSpec((rows, inner), lambda i, m: (0, 0)) for _ in range(shifts)]
        + [pl.BlockSpec((inner, col_width), lambda i, m: (0, m[0] * halves + m[1]))]
        + [pl.BlockSpec((inner, col_width), lambda i, m: (0, m[1])) for _ in received],
        out_specs=pl.BlockSpec((rows, col_width), lambda i, m: (0, 0)),
    )
    return pl.pallas_call(
        functools.partial(project_kernel, shifts=shifts),
        grid_spec=grid_spec,
        out_shape=jax.ShapeDtypeStruct((rows, col_width), out_dtype),
        cost_estimate=pl.CostEstimate(
            flops=2 * rows * inner * shifts * col_width,
            transcendentals=0,
            bytes_accessed=rows * inner * shifts * 2 + shifts * inner * col_width * 2
            + rows * col_width * jnp.dtype(out_dtype).itemsize,
        ),
    )(meta, *pieces, out_weight, *received)


def join_kernel(k_hbm, v_hbm, o_hbm, sems):
    width = k_hbm.shape[1]
    first = pltpu.make_async_copy(k_hbm, o_hbm.at[:, pl.ds(0, width)], sems.at[0])
    second = pltpu.make_async_copy(v_hbm, o_hbm.at[:, pl.ds(width, width)], sems.at[1])
    first.start()
    second.start()
    first.wait()
    second.wait()


def join(key_rows, value_rows):
    rows, width = key_rows.shape
    return pl.pallas_call(
        join_kernel,
        in_specs=[pl.BlockSpec(memory_space=pl.ANY), pl.BlockSpec(memory_space=pl.ANY)],
        out_specs=pl.BlockSpec(memory_space=pl.ANY),
        out_shape=jax.ShapeDtypeStruct((rows, 2 * width), key_rows.dtype),
        scratch_shapes=[pltpu.SemaphoreType.DMA((2,))],
        cost_estimate=pl.CostEstimate(
            flops=0, transcendentals=0, bytes_accessed=4 * key_rows.size * key_rows.dtype.itemsize
        ),
    )(key_rows, value_rows)


def finish_kernel(own_ref, got_ref, o_ref):
    o_ref[...] = (own_ref[...] + got_ref[...].astype(jnp.float32)).astype(o_ref.dtype)


def finish(own, got, chunks=4):
    rows, width = own.shape
    blk = pl.BlockSpec((rows // chunks, width), lambda i: (i, 0))
    return pl.pallas_call(
        finish_kernel,
        grid=(chunks,),
        in_specs=[blk, blk],
        out_specs=blk,
        out_shape=jax.ShapeDtypeStruct((rows, width), got.dtype),
        cost_estimate=pl.CostEstimate(
            flops=own.size, transcendentals=0, bytes_accessed=own.size * 4 + got.size * 4
        ),
    )(own, got)


CTX = ("xl", "z", "core")
TP = ("y", "xh")


def per_device(queries, key_rows, value_rows, selection, out_weight):
    row_count, feat_width = queries.shape
    topk = selection.shape[1]
    y_size = lax.axis_size("y")
    xh_size = lax.axis_size("xh")
    y_place = lax.axis_index("y")
    ctx_place = lax.axis_index(CTX)
    own_choice = lax.dynamic_slice_in_dim(selection, ctx_place, 1, 0)[0]
    meta = jnp.concatenate([own_choice, ctx_place.astype(jnp.int32)[None]])
    kv_piece = lax.all_gather(
        join(key_rows, value_rows), CTX, axis=0, tiled=True
    )
    group_width = out_weight.shape[1] // y_size
    received = []
    for shift in range(1, y_size):
        dest = (y_place + shift) % y_size
        sent = lax.dynamic_slice_in_dim(out_weight, dest * group_width, group_width, 1)
        received.append(
            lax.ppermute(sent, "y", [(i, (i + shift) % y_size) for i in range(y_size)])
        )
    kv_piece, received = lax.optimization_barrier((kv_piece, received))
    attended = attend(meta, queries, kv_piece, topk)
    pieces = [attended] + [
        lax.ppermute(attended, "y", [(i, (i + shift) % y_size) for i in range(y_size)])
        for shift in range(1, y_size)
    ]
    xh_place = lax.axis_index("xh")
    other = jnp.stack([y_place, xh_size - 1 - xh_place]).astype(jnp.int32)
    mine = jnp.stack([y_place, xh_place]).astype(jnp.int32)
    sent = project(other, pieces, out_weight, received, xh_size, queries.dtype)
    got = lax.ppermute(sent, "xh", [(i, xh_size - 1 - i) for i in range(xh_size)])
    own = project(mine, pieces, out_weight, received, xh_size, jnp.float32)
    return finish(own, got)


def solution(mesh):
    ctx_size, tp_size = mesh.devices.shape
    view = Mesh(
        mesh.devices.reshape(2, ctx_size // 4, 2, tp_size // 2, 2), ("xl", "z", "core", "y", "xh")
    )
    placed = (P(CTX, TP), P(CTX, TP), P(CTX, TP), P(), P(TP, None))
    return jax.shard_map(
        per_device, mesh=view, in_specs=placed, out_specs=P(CTX, TP), check_vma=False
    )
```

```python
import functools

import jax
import jax.numpy as jnp
from jax import lax
from jax.experimental import pallas as pl
from jax.experimental.pallas import tpu as pltpu
from jax.sharding import Mesh, PartitionSpec as P

HD = 128
BLOCK = 512

neg_fill = -1e30


def attend_kernel(meta_ref, q_ref, *refs, topk, head_count):
    k_refs = refs[:topk]
    v_refs = refs[topk : 2 * topk]
    att_ref = refs[2 * topk]
    if True:
        scaling = 1.0 / jnp.sqrt(jnp.float32(HD))
        q_block = meta_ref[topk]
        query_pos = q_block * BLOCK + lax.broadcasted_iota(jnp.int32, (BLOCK, BLOCK), 0)
        key_pos = meta_ref[0] * BLOCK + lax.broadcasted_iota(jnp.int32, (BLOCK, BLOCK), 1)
        causal = key_pos <= query_pos
        usable = [None] + [
            (meta_ref[s] != meta_ref[0]) & (meta_ref[s] < q_block) for s in range(1, topk)
        ]
        for h in range(head_count):
            cols = slice(h * HD, (h + 1) * HD)
            q = q_ref[:, cols]
            scores = []
            for s in range(topk):
                sc = lax.dot_general(
                    q, k_refs[s][:, cols], (((1,), (1,)), ((), ())),
                    preferred_element_type=jnp.float32,
                ) * scaling
                if s == 0:
                    sc = jnp.where(causal, sc, neg_fill)
                else:
                    sc = jnp.where(usable[s], sc, neg_fill)
                scores.append(sc)
            row_max = jnp.max(scores[0], axis=1, keepdims=True)
            for s in range(1, topk):
                row_max = jnp.maximum(row_max, jnp.max(scores[s], axis=1, keepdims=True))
            row_sum = jnp.zeros((BLOCK, 1), jnp.float32)
            acc = jnp.zeros((BLOCK, HD), jnp.float32)
            for s in range(topk):
                e = jnp.exp(scores[s] - row_max)
                row_sum = row_sum + jnp.sum(e, axis=1, keepdims=True)
                acc = acc + jnp.dot(
                    e.astype(jnp.bfloat16), v_refs[s][:, cols],
                    preferred_element_type=jnp.float32,
                )
            att_ref[:, cols] = (acc / row_sum).astype(att_ref.dtype)


def project_kernel(y_ref, *refs, shifts):
    a_refs = refs[:shifts]
    w_refs = refs[shifts : 2 * shifts]
    o_ref = refs[2 * shifts]
    acc = jnp.dot(a_refs[0][...], w_refs[0][...], preferred_element_type=jnp.float32)
    for sh in range(1, shifts):
        acc = acc + jnp.dot(a_refs[sh][...], w_refs[sh][...], preferred_element_type=jnp.float32)
    o_ref[...] = acc.astype(o_ref.dtype)


def attend(meta, queries, kv_piece, topk):
    row_count, feat_width = queries.shape
    head_count = feat_width // HD

    def k_map(s):
        return lambda j, m: (m[s], 0)

    def v_map(s):
        return lambda j, m: (m[s], 1)

    blk = (BLOCK, feat_width)
    grid_spec = pltpu.PrefetchScalarGridSpec(
        num_scalar_prefetch=1,
        grid=(1,),
        in_specs=[pl.BlockSpec(blk, lambda j, m: (0, 0))]
        + [pl.BlockSpec(blk, k_map(s)) for s in range(topk)]
        + [pl.BlockSpec(blk, v_map(s)) for s in range(topk)],
        out_specs=pl.BlockSpec(blk, lambda j, m: (0, 0)),
    )
    return pl.pallas_call(
        functools.partial(attend_kernel, topk=topk, head_count=head_count),
        grid_spec=grid_spec,
        out_shape=jax.ShapeDtypeStruct((row_count, feat_width), queries.dtype),
        cost_estimate=pl.CostEstimate(
            flops=4 * head_count * BLOCK * topk * BLOCK * HD,
            transcendentals=head_count * BLOCK * topk * BLOCK,
            bytes_accessed=queries.size * 2 * (2 + 2 * topk),
        ),
    )(meta, queries, *([kv_piece] * (2 * topk)))


def project(meta, pieces, out_weight, received, halves, out_dtype):
    rows, inner = pieces[0].shape
    shifts = len(received) + 1
    col_width = received[0].shape[1] // halves
    grid_spec = pltpu.PrefetchScalarGridSpec(
        num_scalar_prefetch=1,
        grid=(1,),
        in_specs=[pl.BlockSpec((rows, inner), lambda i, m: (0, 0)) for _ in range(shifts)]
        + [pl.BlockSpec((inner, col_width), lambda i, m: (0, m[0] * halves + m[1]))]
        + [pl.BlockSpec((inner, col_width), lambda i, m: (0, m[1])) for _ in received],
        out_specs=pl.BlockSpec((rows, col_width), lambda i, m: (0, 0)),
    )
    return pl.pallas_call(
        functools.partial(project_kernel, shifts=shifts),
        grid_spec=grid_spec,
        out_shape=jax.ShapeDtypeStruct((rows, col_width), out_dtype),
        cost_estimate=pl.CostEstimate(
            flops=2 * rows * inner * shifts * col_width,
            transcendentals=0,
            bytes_accessed=rows * inner * shifts * 2 + shifts * inner * col_width * 2
            + rows * col_width * jnp.dtype(out_dtype).itemsize,
        ),
    )(meta, *pieces, out_weight, *received)


def part_kernel(meta_ref, *refs, count, has_partial):
    start = 1 if has_partial else 0
    a_refs = refs[start : start + count]
    w_refs = refs[start + count : start + 2 * count]
    o_ref = refs[start + 2 * count]
    acc = refs[0][...] if has_partial else None
    for a_ref, w_ref in zip(a_refs, w_refs):
        term = jnp.dot(a_ref[...], w_ref[...], preferred_element_type=jnp.float32)
        acc = term if acc is None else acc + term
    o_ref[...] = acc.astype(o_ref.dtype)


def project_part(meta, partial, pieces, weights, local_first, halves, out_dtype):
    rows, inner = pieces[0].shape
    col_width = weights[-1].shape[1] // halves
    w_specs = [pl.BlockSpec((inner, col_width), lambda i, m: (0, m[1])) for _ in weights]
    if local_first:
        w_specs[0] = pl.BlockSpec((inner, col_width), lambda i, m: (0, m[0] * halves + m[1]))
    full = pl.BlockSpec((rows, col_width), lambda i, m: (0, 0))
    grid_spec = pltpu.PrefetchScalarGridSpec(
        num_scalar_prefetch=1,
        grid=(1,),
        in_specs=([full] if partial is not None else [])
        + [pl.BlockSpec((rows, inner), lambda i, m: (0, 0)) for _ in pieces]
        + w_specs,
        out_specs=full,
    )
    extra = [partial] if partial is not None else []
    return pl.pallas_call(
        functools.partial(part_kernel, count=len(pieces), has_partial=partial is not None),
        grid_spec=grid_spec,
        out_shape=jax.ShapeDtypeStruct((rows, col_width), out_dtype),
        cost_estimate=pl.CostEstimate(
            flops=2 * rows * inner * len(pieces) * col_width,
            transcendentals=0,
            bytes_accessed=rows * inner * len(pieces) * 2 + len(pieces) * inner * col_width * 2
            + rows * col_width * (4 * len(extra) + jnp.dtype(out_dtype).itemsize),
        ),
    )(meta, *extra, *pieces, *weights)


CTX = ("xl", "z", "core")
TP = ("y", "xh")


def per_device(queries, key_rows, value_rows, selection, out_weight):
    row_count, feat_width = queries.shape
    topk = selection.shape[1]
    y_size = lax.axis_size("y")
    xh_size = lax.axis_size("xh")
    y_place = lax.axis_index("y")
    ctx_place = lax.axis_index(CTX)
    own_choice = lax.dynamic_slice_in_dim(selection, ctx_place, 1, 0)[0]
    meta = jnp.concatenate([own_choice, ctx_place.astype(jnp.int32)[None]])
    kv_piece = lax.all_gather(
        jnp.concatenate([key_rows, value_rows], axis=1), CTX, axis=0, tiled=True
    )
    group_width = out_weight.shape[1] // y_size
    received = []
    for shift in range(1, y_size):
        dest = (y_place + shift) % y_size
        sent = lax.dynamic_slice_in_dim(out_weight, dest * group_width, group_width, 1)
        received.append(
            lax.ppermute(sent, "y", [(i, (i + shift) % y_size) for i in range(y_size)])
        )
    kv_piece, received = lax.optimization_barrier((kv_piece, received))
    attended = attend(meta, queries, kv_piece, topk)
    pieces = [attended] + [
        lax.ppermute(attended, "y", [(i, (i + shift) % y_size) for i in range(y_size)])
        for shift in range(1, y_size)
    ]
    xh_place = lax.axis_index("xh")
    other = jnp.stack([y_place, xh_size - 1 - xh_place]).astype(jnp.int32)
    mine = jnp.stack([y_place, xh_place]).astype(jnp.int32)
    early = project_part(
        other, None, pieces[:2], [out_weight, received[0]], True, xh_size, jnp.float32
    )
    sent = project_part(
        other, early, pieces[2:], list(received[1:]), False, xh_size, queries.dtype
    )
    got = lax.ppermute(sent, "xh", [(i, xh_size - 1 - i) for i in range(xh_size)])
    own = project(mine, pieces, out_weight, received, xh_size, jnp.float32)
    return (own + got.astype(jnp.float32)).astype(queries.dtype)


def solution(mesh):
    ctx_size, tp_size = mesh.devices.shape
    view = Mesh(
        mesh.devices.reshape(2, ctx_size // 4, 2, tp_size // 2, 2), ("xl", "z", "core", "y", "xh")
    )
    placed = (P(CTX, TP), P(CTX, TP), P(CTX, TP), P(), P(TP, None))
    return jax.shard_map(
        per_device, mesh=view, in_specs=placed, out_specs=P(CTX, TP), check_vma=False
    )
```

```python
import functools

import jax
import jax.numpy as jnp
from jax import lax
from jax.experimental import pallas as pl
from jax.experimental.pallas import tpu as pltpu
from jax.sharding import Mesh, PartitionSpec as P

HD = 128
BLOCK = 512

neg_fill = -1e30


def attend_kernel(meta_ref, q_ref, *refs, topk, head_count):
    k_refs = refs[:topk]
    v_refs = refs[topk : 2 * topk]
    att_ref = refs[2 * topk]
    if True:
        scaling = 1.0 / jnp.sqrt(jnp.float32(HD))
        q_block = meta_ref[topk]
        query_pos = q_block * BLOCK + lax.broadcasted_iota(jnp.int32, (BLOCK, BLOCK), 0)
        key_pos = meta_ref[0] * BLOCK + lax.broadcasted_iota(jnp.int32, (BLOCK, BLOCK), 1)
        causal = key_pos <= query_pos
        usable = [None] + [
            (meta_ref[s] != meta_ref[0]) & (meta_ref[s] < q_block) for s in range(1, topk)
        ]
        for h in range(head_count):
            cols = slice(h * HD, (h + 1) * HD)
            q = q_ref[:, cols]
            scores = []
            for s in range(topk):
                sc = lax.dot_general(
                    q, k_refs[s][:, cols], (((1,), (1,)), ((), ())),
                    preferred_element_type=jnp.float32,
                ) * scaling
                if s == 0:
                    sc = jnp.where(causal, sc, neg_fill)
                else:
                    sc = jnp.where(usable[s], sc, neg_fill)
                scores.append(sc)
            row_max = jnp.max(scores[0], axis=1, keepdims=True)
            for s in range(1, topk):
                row_max = jnp.maximum(row_max, jnp.max(scores[s], axis=1, keepdims=True))
            row_sum = jnp.zeros((BLOCK, 1), jnp.float32)
            acc = jnp.zeros((BLOCK, HD), jnp.float32)
            for s in range(topk):
                e = jnp.exp(scores[s] - row_max)
                row_sum = row_sum + jnp.sum(e, axis=1, keepdims=True)
                acc = acc + jnp.dot(
                    e.astype(jnp.bfloat16), v_refs[s][:, cols],
                    preferred_element_type=jnp.float32,
                )
            att_ref[:, cols] = (acc / row_sum).astype(att_ref.dtype)


def project_kernel(y_ref, *refs, shifts):
    a_refs = refs[:shifts]
    w_refs = refs[shifts : 2 * shifts]
    o_ref = refs[2 * shifts]
    acc = jnp.dot(a_refs[0][...], w_refs[0][...], preferred_element_type=jnp.float32)
    for sh in range(1, shifts):
        acc = acc + jnp.dot(a_refs[sh][...], w_refs[sh][...], preferred_element_type=jnp.float32)
    o_ref[...] = acc.astype(o_ref.dtype)


def attend(meta, queries, kv_piece, topk):
    row_count, feat_width = queries.shape
    head_count = feat_width // HD

    def k_map(s):
        return lambda j, m: (m[s], 0)

    def v_map(s):
        return lambda j, m: (m[s], 1)

    blk = (BLOCK, feat_width)
    grid_spec = pltpu.PrefetchScalarGridSpec(
        num_scalar_prefetch=1,
        grid=(1,),
        in_specs=[pl.BlockSpec(blk, lambda j, m: (0, 0))]
        + [pl.BlockSpec(blk, k_map(s)) for s in range(topk)]
        + [pl.BlockSpec(blk, v_map(s)) for s in range(topk)],
        out_specs=pl.BlockSpec(blk, lambda j, m: (0, 0)),
    )
    return pl.pallas_call(
        functools.partial(attend_kernel, topk=topk, head_count=head_count),
        grid_spec=grid_spec,
        out_shape=jax.ShapeDtypeStruct((row_count, feat_width), queries.dtype),
        cost_estimate=pl.CostEstimate(
            flops=4 * head_count * BLOCK * topk * BLOCK * HD,
            transcendentals=head_count * BLOCK * topk * BLOCK,
            bytes_accessed=queries.size * 2 * (2 + 2 * topk),
        ),
    )(meta, queries, *([kv_piece] * (2 * topk)))


def project(meta, pieces, out_weight, received, halves, out_dtype):
    rows, inner = pieces[0].shape
    shifts = len(received) + 1
    col_width = received[0].shape[1] // halves
    grid_spec = pltpu.PrefetchScalarGridSpec(
        num_scalar_prefetch=1,
        grid=(1,),
        in_specs=[pl.BlockSpec((rows, inner), lambda i, m: (0, 0)) for _ in range(shifts)]
        + [pl.BlockSpec((inner, col_width), lambda i, m: (0, m[0] * halves + m[1]))]
        + [pl.BlockSpec((inner, col_width), lambda i, m: (0, m[1])) for _ in received],
        out_specs=pl.BlockSpec((rows, col_width), lambda i, m: (0, 0)),
    )
    return pl.pallas_call(
        functools.partial(project_kernel, shifts=shifts),
        grid_spec=grid_spec,
        out_shape=jax.ShapeDtypeStruct((rows, col_width), out_dtype),
        cost_estimate=pl.CostEstimate(
            flops=2 * rows * inner * shifts * col_width,
            transcendentals=0,
            bytes_accessed=rows * inner * shifts * 2 + shifts * inner * col_width * 2
            + rows * col_width * jnp.dtype(out_dtype).itemsize,
        ),
    )(meta, *pieces, out_weight, *received)


def part_kernel(meta_ref, *refs, count, has_partial):
    start = 1 if has_partial else 0
    a_refs = refs[start : start + count]
    w_refs = refs[start + count : start + 2 * count]
    o_ref = refs[start + 2 * count]
    acc = refs[0][...] if has_partial else None
    for a_ref, w_ref in zip(a_refs, w_refs):
        term = jnp.dot(a_ref[...], w_ref[...], preferred_element_type=jnp.float32)
        acc = term if acc is None else acc + term
    o_ref[...] = acc.astype(o_ref.dtype)


def project_part(meta, partial, pieces, weights, local_first, halves, out_dtype):
    rows, inner = pieces[0].shape
    col_width = weights[-1].shape[1] // halves
    w_specs = [pl.BlockSpec((inner, col_width), lambda i, m: (0, m[1])) for _ in weights]
    if local_first:
        w_specs[0] = pl.BlockSpec((inner, col_width), lambda i, m: (0, m[0] * halves + m[1]))
    full = pl.BlockSpec((rows, col_width), lambda i, m: (0, 0))
    grid_spec = pltpu.PrefetchScalarGridSpec(
        num_scalar_prefetch=1,
        grid=(1,),
        in_specs=([full] if partial is not None else [])
        + [pl.BlockSpec((rows, inner), lambda i, m: (0, 0)) for _ in pieces]
        + w_specs,
        out_specs=full,
    )
    extra = [partial] if partial is not None else []
    return pl.pallas_call(
        functools.partial(part_kernel, count=len(pieces), has_partial=partial is not None),
        grid_spec=grid_spec,
        out_shape=jax.ShapeDtypeStruct((rows, col_width), out_dtype),
        cost_estimate=pl.CostEstimate(
            flops=2 * rows * inner * len(pieces) * col_width,
            transcendentals=0,
            bytes_accessed=rows * inner * len(pieces) * 2 + len(pieces) * inner * col_width * 2
            + rows * col_width * (4 * len(extra) + jnp.dtype(out_dtype).itemsize),
        ),
    )(meta, *extra, *pieces, *weights)


def join_kernel(k_ref, v_ref, o_ref):
    width = k_ref.shape[1]
    o_ref[:, :width] = k_ref[...]
    o_ref[:, width:] = v_ref[...]


def join(key_rows, value_rows, chunks=4):
    rows, width = key_rows.shape
    part = pl.BlockSpec((rows // chunks, width), lambda i: (i, 0))
    return pl.pallas_call(
        join_kernel,
        grid=(chunks,),
        in_specs=[part, part],
        out_specs=pl.BlockSpec((rows // chunks, 2 * width), lambda i: (i, 0)),
        out_shape=jax.ShapeDtypeStruct((rows, 2 * width), key_rows.dtype),
        cost_estimate=pl.CostEstimate(
            flops=0, transcendentals=0, bytes_accessed=4 * key_rows.size * key_rows.dtype.itemsize
        ),
    )(key_rows, value_rows)


CTX = ("xl", "z", "core")
TP = ("y", "xh")


def per_device(queries, key_rows, value_rows, selection, out_weight):
    row_count, feat_width = queries.shape
    topk = selection.shape[1]
    y_size = lax.axis_size("y")
    xh_size = lax.axis_size("xh")
    y_place = lax.axis_index("y")
    ctx_place = lax.axis_index(CTX)
    own_choice = lax.dynamic_slice_in_dim(selection, ctx_place, 1, 0)[0]
    meta = jnp.concatenate([own_choice, ctx_place.astype(jnp.int32)[None]])
    kv_piece = lax.all_gather(
        join(key_rows, value_rows), CTX, axis=0, tiled=True
    )
    group_width = out_weight.shape[1] // y_size
    received = []
    for shift in range(1, y_size):
        dest = (y_place + shift) % y_size
        sent = lax.dynamic_slice_in_dim(out_weight, dest * group_width, group_width, 1)
        received.append(
            lax.ppermute(sent, "y", [(i, (i + shift) % y_size) for i in range(y_size)])
        )
    kv_piece, received = lax.optimization_barrier((kv_piece, received))
    attended = attend(meta, queries, kv_piece, topk)
    pieces = [attended] + [
        lax.ppermute(attended, "y", [(i, (i + shift) % y_size) for i in range(y_size)])
        for shift in range(1, y_size)
    ]
    xh_place = lax.axis_index("xh")
    other = jnp.stack([y_place, xh_size - 1 - xh_place]).astype(jnp.int32)
    mine = jnp.stack([y_place, xh_place]).astype(jnp.int32)
    early = project_part(
        other, None, pieces[:2], [out_weight, received[0]], True, xh_size, jnp.float32
    )
    sent = project_part(
        other, early, pieces[2:], list(received[1:]), False, xh_size, queries.dtype
    )
    got = lax.ppermute(sent, "xh", [(i, xh_size - 1 - i) for i in range(xh_size)])
    own = project(mine, pieces, out_weight, received, xh_size, jnp.float32)
    return (own + got.astype(jnp.float32)).astype(queries.dtype)


def solution(mesh):
    ctx_size, tp_size = mesh.devices.shape
    view = Mesh(
        mesh.devices.reshape(2, ctx_size // 4, 2, tp_size // 2, 2), ("xl", "z", "core", "y", "xh")
    )
    placed = (P(CTX, TP), P(CTX, TP), P(CTX, TP), P(), P(TP, None))
    return jax.shard_map(
        per_device, mesh=view, in_specs=placed, out_specs=P(CTX, TP), check_vma=False
    )
```

```python
import functools

import jax
import jax.numpy as jnp
from jax import lax
from jax.experimental import pallas as pl
from jax.experimental.pallas import tpu as pltpu
from jax.sharding import Mesh, PartitionSpec as P

HD = 128
BLOCK = 512

neg_fill = -1e30


def attend_kernel(meta_ref, q_ref, *refs, topk, head_count):
    k_refs = refs[:topk]
    v_refs = refs[topk : 2 * topk]
    att_ref = refs[2 * topk]
    if True:
        scaling = 1.0 / jnp.sqrt(jnp.float32(HD))
        q_block = meta_ref[topk]
        query_pos = q_block * BLOCK + lax.broadcasted_iota(jnp.int32, (BLOCK, BLOCK), 0)
        key_pos = meta_ref[0] * BLOCK + lax.broadcasted_iota(jnp.int32, (BLOCK, BLOCK), 1)
        causal = key_pos <= query_pos
        usable = [None] + [
            (meta_ref[s] != meta_ref[0]) & (meta_ref[s] < q_block) for s in range(1, topk)
        ]
        for h in range(head_count):
            cols = slice(h * HD, (h + 1) * HD)
            q = q_ref[:, cols]
            scores = []
            for s in range(topk):
                sc = lax.dot_general(
                    q, k_refs[s][:, cols], (((1,), (1,)), ((), ())),
                    preferred_element_type=jnp.float32,
                ) * scaling
                if s == 0:
                    sc = jnp.where(causal, sc, neg_fill)
                else:
                    sc = jnp.where(usable[s], sc, neg_fill)
                scores.append(sc)
            row_max = jnp.max(scores[0], axis=1, keepdims=True)
            for s in range(1, topk):
                row_max = jnp.maximum(row_max, jnp.max(scores[s], axis=1, keepdims=True))
            row_sum = jnp.zeros((BLOCK, 1), jnp.float32)
            acc = jnp.zeros((BLOCK, HD), jnp.float32)
            for s in range(topk):
                e = jnp.exp(scores[s] - row_max)
                row_sum = row_sum + jnp.sum(e, axis=1, keepdims=True)
                acc = acc + jnp.dot(
                    e.astype(jnp.bfloat16), v_refs[s][:, cols],
                    preferred_element_type=jnp.float32,
                )
            att_ref[:, cols] = (acc / row_sum).astype(att_ref.dtype)


def project_kernel(y_ref, *refs, shifts):
    a_refs = refs[:shifts]
    w_refs = refs[shifts : 2 * shifts]
    o_ref = refs[2 * shifts]
    acc = jnp.dot(a_refs[0][...], w_refs[0][...], preferred_element_type=jnp.float32)
    for sh in range(1, shifts):
        acc = acc + jnp.dot(a_refs[sh][...], w_refs[sh][...], preferred_element_type=jnp.float32)
    o_ref[...] = acc.astype(o_ref.dtype)


def attend(meta, queries, kv_piece, topk):
    row_count, feat_width = queries.shape
    head_count = feat_width // HD

    def k_map(s):
        return lambda j, m: (m[s], 0)

    def v_map(s):
        return lambda j, m: (m[s], 1)

    blk = (BLOCK, feat_width)
    grid_spec = pltpu.PrefetchScalarGridSpec(
        num_scalar_prefetch=1,
        grid=(1,),
        in_specs=[pl.BlockSpec(blk, lambda j, m: (0, 0))]
        + [pl.BlockSpec(blk, k_map(s)) for s in range(topk)]
        + [pl.BlockSpec(blk, v_map(s)) for s in range(topk)],
        out_specs=pl.BlockSpec(blk, lambda j, m: (0, 0)),
    )
    return pl.pallas_call(
        functools.partial(attend_kernel, topk=topk, head_count=head_count),
        grid_spec=grid_spec,
        out_shape=jax.ShapeDtypeStruct((row_count, feat_width), queries.dtype),
        cost_estimate=pl.CostEstimate(
            flops=4 * head_count * BLOCK * topk * BLOCK * HD,
            transcendentals=head_count * BLOCK * topk * BLOCK,
            bytes_accessed=queries.size * 2 * (2 + 2 * topk),
        ),
    )(meta, queries, *([kv_piece] * (2 * topk)))


def project(meta, pieces, out_weight, received, halves, out_dtype):
    rows, inner = pieces[0].shape
    shifts = len(received) + 1
    col_width = received[0].shape[1] // halves
    grid_spec = pltpu.PrefetchScalarGridSpec(
        num_scalar_prefetch=1,
        grid=(1,),
        in_specs=[pl.BlockSpec((rows, inner), lambda i, m: (0, 0)) for _ in range(shifts)]
        + [pl.BlockSpec((inner, col_width), lambda i, m: (0, m[0] * halves + m[1]))]
        + [pl.BlockSpec((inner, col_width), lambda i, m: (0, m[1])) for _ in received],
        out_specs=pl.BlockSpec((rows, col_width), lambda i, m: (0, 0)),
    )
    return pl.pallas_call(
        functools.partial(project_kernel, shifts=shifts),
        grid_spec=grid_spec,
        out_shape=jax.ShapeDtypeStruct((rows, col_width), out_dtype),
        cost_estimate=pl.CostEstimate(
            flops=2 * rows * inner * shifts * col_width,
            transcendentals=0,
            bytes_accessed=rows * inner * shifts * 2 + shifts * inner * col_width * 2
            + rows * col_width * jnp.dtype(out_dtype).itemsize,
        ),
    )(meta, *pieces, out_weight, *received)


def part_kernel(meta_ref, *refs, count, has_partial):
    start = 1 if has_partial else 0
    a_refs = refs[start : start + count]
    w_refs = refs[start + count : start + 2 * count]
    o_ref = refs[start + 2 * count]
    acc = refs[0][...] if has_partial else None
    for a_ref, w_ref in zip(a_refs, w_refs):
        term = jnp.dot(a_ref[...], w_ref[...], preferred_element_type=jnp.float32)
        acc = term if acc is None else acc + term
    o_ref[...] = acc.astype(o_ref.dtype)


def project_part(meta, partial, pieces, weights, local_first, halves, out_dtype):
    rows, inner = pieces[0].shape
    col_width = weights[-1].shape[1] // halves
    w_specs = [pl.BlockSpec((inner, col_width), lambda i, m: (0, m[1])) for _ in weights]
    if local_first:
        w_specs[0] = pl.BlockSpec((inner, col_width), lambda i, m: (0, m[0] * halves + m[1]))
    full = pl.BlockSpec((rows, col_width), lambda i, m: (0, 0))
    grid_spec = pltpu.PrefetchScalarGridSpec(
        num_scalar_prefetch=1,
        grid=(1,),
        in_specs=([full] if partial is not None else [])
        + [pl.BlockSpec((rows, inner), lambda i, m: (0, 0)) for _ in pieces]
        + w_specs,
        out_specs=full,
    )
    extra = [partial] if partial is not None else []
    return pl.pallas_call(
        functools.partial(part_kernel, count=len(pieces), has_partial=partial is not None),
        grid_spec=grid_spec,
        out_shape=jax.ShapeDtypeStruct((rows, col_width), out_dtype),
        cost_estimate=pl.CostEstimate(
            flops=2 * rows * inner * len(pieces) * col_width,
            transcendentals=0,
            bytes_accessed=rows * inner * len(pieces) * 2 + len(pieces) * inner * col_width * 2
            + rows * col_width * (4 * len(extra) + jnp.dtype(out_dtype).itemsize),
        ),
    )(meta, *extra, *pieces, *weights)


CTX = ("xl", "z", "core")
TP = ("y", "xh")


def per_device(queries, key_rows, value_rows, selection, out_weight):
    row_count, feat_width = queries.shape
    topk = selection.shape[1]
    y_size = lax.axis_size("y")
    xh_size = lax.axis_size("xh")
    y_place = lax.axis_index("y")
    ctx_place = lax.axis_index(CTX)
    own_choice = lax.dynamic_slice_in_dim(selection, ctx_place, 1, 0)[0]
    meta = jnp.concatenate([own_choice, ctx_place.astype(jnp.int32)[None]])
    kv_piece = lax.all_gather(
        jnp.concatenate([key_rows, value_rows], axis=1), CTX, axis=0, tiled=True
    )
    group_width = out_weight.shape[1] // y_size
    received = []
    for shift in range(1, y_size):
        dest = (y_place + shift) % y_size
        sent = lax.dynamic_slice_in_dim(out_weight, dest * group_width, group_width, 1)
        received.append(
            lax.ppermute(sent, "y", [(i, (i + shift) % y_size) for i in range(y_size)])
        )
    kv_piece, received = lax.optimization_barrier((kv_piece, received))
    attended = attend(meta, queries, kv_piece, topk)
    pieces = [attended] + [
        lax.ppermute(attended, "y", [(i, (i + shift) % y_size) for i in range(y_size)])
        for shift in range(1, y_size)
    ]
    xh_place = lax.axis_index("xh")
    other = jnp.stack([y_place, xh_size - 1 - xh_place]).astype(jnp.int32)
    mine = jnp.stack([y_place, xh_place]).astype(jnp.int32)
    early = project_part(
        other, None, pieces[:2], [out_weight, received[0]], True, xh_size, jnp.float32
    )
    near = project_part(
        other, early, pieces[3:], list(received[2:]), False, xh_size, jnp.float32
    )
    sent = project_part(
        other, near, pieces[2:3], list(received[1:2]), False, xh_size, queries.dtype
    )
    got = lax.ppermute(sent, "xh", [(i, xh_size - 1 - i) for i in range(xh_size)])
    own = project(mine, pieces, out_weight, received, xh_size, jnp.float32)
    return (own + got.astype(jnp.float32)).astype(queries.dtype)


def solution(mesh):
    ctx_size, tp_size = mesh.devices.shape
    view = Mesh(
        mesh.devices.reshape(2, ctx_size // 4, 2, tp_size // 2, 2), ("xl", "z", "core", "y", "xh")
    )
    placed = (P(CTX, TP), P(CTX, TP), P(CTX, TP), P(), P(TP, None))
    return jax.shard_map(
        per_device, mesh=view, in_specs=placed, out_specs=P(CTX, TP), check_vma=False
    )
```

```python
import functools

import jax
import jax.numpy as jnp
from jax import lax
from jax.experimental import pallas as pl
from jax.experimental.pallas import tpu as pltpu
from jax.sharding import Mesh, PartitionSpec as P

HD = 128
BLOCK = 512

neg_fill = -1e30


def attend_kernel(meta_ref, q_ref, *refs, topk, head_count):
    k_refs = refs[:topk]
    v_refs = refs[topk : 2 * topk]
    att_ref = refs[2 * topk]
    if True:
        scaling = 1.0 / jnp.sqrt(jnp.float32(HD))
        q_block = meta_ref[topk]
        query_pos = q_block * BLOCK + lax.broadcasted_iota(jnp.int32, (BLOCK, BLOCK), 0)
        key_pos = meta_ref[0] * BLOCK + lax.broadcasted_iota(jnp.int32, (BLOCK, BLOCK), 1)
        causal = key_pos <= query_pos
        usable = [None] + [
            (meta_ref[s] != meta_ref[0]) & (meta_ref[s] < q_block) for s in range(1, topk)
        ]
        for h in range(head_count):
            cols = slice(h * HD, (h + 1) * HD)
            q = q_ref[:, cols]
            scores = []
            for s in range(topk):
                sc = lax.dot_general(
                    q, k_refs[s][:, cols], (((1,), (1,)), ((), ())),
                    preferred_element_type=jnp.float32,
                ) * scaling
                if s == 0:
                    sc = jnp.where(causal, sc, neg_fill)
                else:
                    sc = jnp.where(usable[s], sc, neg_fill)
                scores.append(sc)
            row_max = jnp.max(scores[0], axis=1, keepdims=True)
            for s in range(1, topk):
                row_max = jnp.maximum(row_max, jnp.max(scores[s], axis=1, keepdims=True))
            row_sum = jnp.zeros((BLOCK, 1), jnp.float32)
            acc = jnp.zeros((BLOCK, HD), jnp.float32)
            for s in range(topk):
                e = jnp.exp(scores[s] - row_max)
                row_sum = row_sum + jnp.sum(e, axis=1, keepdims=True)
                acc = acc + jnp.dot(
                    e.astype(jnp.bfloat16), v_refs[s][:, cols],
                    preferred_element_type=jnp.float32,
                )
            att_ref[:, cols] = (acc / row_sum).astype(att_ref.dtype)


def project_kernel(y_ref, *refs, shifts):
    a_refs = refs[:shifts]
    w_refs = refs[shifts : 2 * shifts]
    o_ref = refs[2 * shifts]
    acc = jnp.dot(a_refs[0][...], w_refs[0][...], preferred_element_type=jnp.float32)
    for sh in range(1, shifts):
        acc = acc + jnp.dot(a_refs[sh][...], w_refs[sh][...], preferred_element_type=jnp.float32)
    o_ref[...] = acc.astype(o_ref.dtype)


def attend(meta, queries, kv_piece, topk):
    row_count, feat_width = queries.shape
    head_count = feat_width // HD

    def k_map(s):
        return lambda j, m: (m[s], 0)

    def v_map(s):
        return lambda j, m: (m[s], 1)

    blk = (BLOCK, feat_width)
    grid_spec = pltpu.PrefetchScalarGridSpec(
        num_scalar_prefetch=1,
        grid=(1,),
        in_specs=[pl.BlockSpec(blk, lambda j, m: (0, 0))]
        + [pl.BlockSpec(blk, k_map(s)) for s in range(topk)]
        + [pl.BlockSpec(blk, v_map(s)) for s in range(topk)],
        out_specs=pl.BlockSpec(blk, lambda j, m: (0, 0)),
    )
    return pl.pallas_call(
        functools.partial(attend_kernel, topk=topk, head_count=head_count),
        grid_spec=grid_spec,
        out_shape=jax.ShapeDtypeStruct((row_count, feat_width), queries.dtype),
        cost_estimate=pl.CostEstimate(
            flops=4 * head_count * BLOCK * topk * BLOCK * HD,
            transcendentals=head_count * BLOCK * topk * BLOCK,
            bytes_accessed=queries.size * 2 * (2 + 2 * topk),
        ),
    )(meta, queries, *([kv_piece] * (2 * topk)))


def project(meta, pieces, out_weight, received, halves, out_dtype):
    rows, inner = pieces[0].shape
    shifts = len(received) + 1
    col_width = received[0].shape[1] // halves
    grid_spec = pltpu.PrefetchScalarGridSpec(
        num_scalar_prefetch=1,
        grid=(1,),
        in_specs=[pl.BlockSpec((rows, inner), lambda i, m: (0, 0)) for _ in range(shifts)]
        + [pl.BlockSpec((inner, col_width), lambda i, m: (0, m[0] * halves + m[1]))]
        + [pl.BlockSpec((inner, col_width), lambda i, m: (0, m[1])) for _ in received],
        out_specs=pl.BlockSpec((rows, col_width), lambda i, m: (0, 0)),
    )
    return pl.pallas_call(
        functools.partial(project_kernel, shifts=shifts),
        grid_spec=grid_spec,
        out_shape=jax.ShapeDtypeStruct((rows, col_width), out_dtype),
        cost_estimate=pl.CostEstimate(
            flops=2 * rows * inner * shifts * col_width,
            transcendentals=0,
            bytes_accessed=rows * inner * shifts * 2 + shifts * inner * col_width * 2
            + rows * col_width * jnp.dtype(out_dtype).itemsize,
        ),
    )(meta, *pieces, out_weight, *received)


def part_kernel(meta_ref, *refs, count, has_partial):
    start = 1 if has_partial else 0
    a_refs = refs[start : start + count]
    w_refs = refs[start + count : start + 2 * count]
    o_ref = refs[start + 2 * count]
    acc = refs[0][...] if has_partial else None
    for a_ref, w_ref in zip(a_refs, w_refs):
        term = jnp.dot(a_ref[...], w_ref[...], preferred_element_type=jnp.float32)
        acc = term if acc is None else acc + term
    o_ref[...] = acc.astype(o_ref.dtype)


def project_part(meta, partial, pieces, weights, local_first, halves, out_dtype, part=(0, 1)):
    rows, inner = pieces[0].shape
    rows = rows // part[1]
    col_width = weights[-1].shape[1] // halves
    w_specs = [pl.BlockSpec((inner, col_width), lambda i, m: (0, m[1])) for _ in weights]
    if local_first:
        w_specs[0] = pl.BlockSpec((inner, col_width), lambda i, m: (0, m[0] * halves + m[1]))
    full = pl.BlockSpec((rows, col_width), lambda i, m: (part[0], 0))
    grid_spec = pltpu.PrefetchScalarGridSpec(
        num_scalar_prefetch=1,
        grid=(1,),
        in_specs=([full] if partial is not None else [])
        + [pl.BlockSpec((rows, inner), lambda i, m: (part[0], 0)) for _ in pieces]
        + w_specs,
        out_specs=pl.BlockSpec((rows, col_width), lambda i, m: (0, 0)),
    )
    extra = [partial] if partial is not None else []
    return pl.pallas_call(
        functools.partial(part_kernel, count=len(pieces), has_partial=partial is not None),
        grid_spec=grid_spec,
        out_shape=jax.ShapeDtypeStruct((rows, col_width), out_dtype),
        cost_estimate=pl.CostEstimate(
            flops=2 * rows * inner * len(pieces) * col_width,
            transcendentals=0,
            bytes_accessed=rows * inner * len(pieces) * 2 + len(pieces) * inner * col_width * 2
            + rows * col_width * (4 * len(extra) + jnp.dtype(out_dtype).itemsize),
        ),
    )(meta, *extra, *pieces, *weights)


CTX = ("xl", "z", "core")
TP = ("y", "xh")


def per_device(queries, key_rows, value_rows, selection, out_weight):
    row_count, feat_width = queries.shape
    topk = selection.shape[1]
    y_size = lax.axis_size("y")
    xh_size = lax.axis_size("xh")
    y_place = lax.axis_index("y")
    ctx_place = lax.axis_index(CTX)
    own_choice = lax.dynamic_slice_in_dim(selection, ctx_place, 1, 0)[0]
    meta = jnp.concatenate([own_choice, ctx_place.astype(jnp.int32)[None]])
    kv_piece = lax.all_gather(
        jnp.concatenate([key_rows, value_rows], axis=1), CTX, axis=0, tiled=True
    )
    group_width = out_weight.shape[1] // y_size
    received = []
    for shift in range(1, y_size):
        dest = (y_place + shift) % y_size
        sent = lax.dynamic_slice_in_dim(out_weight, dest * group_width, group_width, 1)
        received.append(
            lax.ppermute(sent, "y", [(i, (i + shift) % y_size) for i in range(y_size)])
        )
    kv_piece, received = lax.optimization_barrier((kv_piece, received))
    attended = attend(meta, queries, kv_piece, topk)
    pieces = [attended] + [
        lax.ppermute(attended, "y", [(i, (i + shift) % y_size) for i in range(y_size)])
        for shift in range(1, y_size)
    ]
    xh_place = lax.axis_index("xh")
    other = jnp.stack([y_place, xh_size - 1 - xh_place]).astype(jnp.int32)
    mine = jnp.stack([y_place, xh_place]).astype(jnp.int32)
    early = project_part(
        other, None, pieces[:2], [out_weight, received[0]], True, xh_size, jnp.float32
    )
    near = project_part(
        other, early, pieces[3:], list(received[2:]), False, xh_size, jnp.float32
    )
    swap = [(i, xh_size - 1 - i) for i in range(xh_size)]
    got = [
        lax.ppermute(
            project_part(
                other, near, pieces[2:3], list(received[1:2]), False, xh_size, queries.dtype,
                (r, 2),
            ),
            "xh",
            swap,
        )
        for r in range(2)
    ]
    got = jnp.concatenate(got)
    own = project(mine, pieces, out_weight, received, xh_size, jnp.float32)
    return (own + got.astype(jnp.float32)).astype(queries.dtype)


def solution(mesh):
    ctx_size, tp_size = mesh.devices.shape
    view = Mesh(
        mesh.devices.reshape(2, ctx_size // 4, 2, tp_size // 2, 2), ("xl", "z", "core", "y", "xh")
    )
    placed = (P(CTX, TP), P(CTX, TP), P(CTX, TP), P(), P(TP, None))
    return jax.shard_map(
        per_device, mesh=view, in_specs=placed, out_specs=P(CTX, TP), check_vma=False
    )
```

```python
import functools

import jax
import jax.numpy as jnp
from jax import lax
from jax.experimental import pallas as pl
from jax.experimental.pallas import tpu as pltpu
from jax.sharding import Mesh, PartitionSpec as P

HD = 128
BLOCK = 512

neg_fill = -1e30


def attend_kernel(meta_ref, q_ref, *refs, topk, head_count):
    k_refs = refs[:topk]
    v_refs = refs[topk : 2 * topk]
    att_ref = refs[2 * topk]
    if True:
        scaling = 1.0 / jnp.sqrt(jnp.float32(HD))
        q_block = meta_ref[topk]
        query_pos = q_block * BLOCK + lax.broadcasted_iota(jnp.int32, (BLOCK, BLOCK), 0)
        key_pos = meta_ref[0] * BLOCK + lax.broadcasted_iota(jnp.int32, (BLOCK, BLOCK), 1)
        causal = key_pos <= query_pos
        usable = [None] + [
            (meta_ref[s] != meta_ref[0]) & (meta_ref[s] < q_block) for s in range(1, topk)
        ]
        for h in range(head_count):
            cols = slice(h * HD, (h + 1) * HD)
            q = q_ref[:, cols]
            scores = []
            for s in range(topk):
                sc = lax.dot_general(
                    q, k_refs[s][:, cols], (((1,), (1,)), ((), ())),
                    preferred_element_type=jnp.float32,
                ) * scaling
                if s == 0:
                    sc = jnp.where(causal, sc, neg_fill)
                else:
                    sc = jnp.where(usable[s], sc, neg_fill)
                scores.append(sc)
            row_max = jnp.max(scores[0], axis=1, keepdims=True)
            for s in range(1, topk):
                row_max = jnp.maximum(row_max, jnp.max(scores[s], axis=1, keepdims=True))
            row_sum = jnp.zeros((BLOCK, 1), jnp.float32)
            acc = jnp.zeros((BLOCK, HD), jnp.float32)
            for s in range(topk):
                e = jnp.exp(scores[s] - row_max)
                row_sum = row_sum + jnp.sum(e, axis=1, keepdims=True)
                acc = acc + jnp.dot(
                    e.astype(jnp.bfloat16), v_refs[s][:, cols],
                    preferred_element_type=jnp.float32,
                )
            att_ref[:, cols] = (acc / row_sum).astype(att_ref.dtype)


def attend(meta, queries, kv_piece, topk, half, parts):
    row_count, feat_width = queries.shape
    width = feat_width // parts
    head_count = width // HD

    def k_map(s):
        return lambda j, m: (m[s], half)

    def v_map(s):
        return lambda j, m: (m[s], parts + half)

    blk = (BLOCK, width)
    grid_spec = pltpu.PrefetchScalarGridSpec(
        num_scalar_prefetch=1,
        grid=(1,),
        in_specs=[pl.BlockSpec(blk, lambda j, m: (0, half))]
        + [pl.BlockSpec(blk, k_map(s)) for s in range(topk)]
        + [pl.BlockSpec(blk, v_map(s)) for s in range(topk)],
        out_specs=pl.BlockSpec(blk, lambda j, m: (0, 0)),
    )
    return pl.pallas_call(
        functools.partial(attend_kernel, topk=topk, head_count=head_count),
        grid_spec=grid_spec,
        out_shape=jax.ShapeDtypeStruct((row_count, width), queries.dtype),
        cost_estimate=pl.CostEstimate(
            flops=4 * head_count * BLOCK * topk * BLOCK * HD,
            transcendentals=head_count * BLOCK * topk * BLOCK,
            bytes_accessed=row_count * width * 2 * (2 + 2 * topk),
        ),
    )(meta, queries, *([kv_piece] * (2 * topk)))


def part_kernel(meta_ref, *refs, count, has_partial):
    start = 1 if has_partial else 0
    a_refs = refs[start : start + count]
    w_refs = refs[start + count : start + 2 * count]
    o_ref = refs[start + 2 * count]
    acc = refs[0][...] if has_partial else None
    for a_ref, w_ref in zip(a_refs, w_refs):
        term = jnp.dot(a_ref[...], w_ref[...], preferred_element_type=jnp.float32)
        acc = term if acc is None else acc + term
    o_ref[...] = acc.astype(o_ref.dtype)


def project_part(meta, partial, terms, halves, out_dtype, part=(0, 1)):
    rows, inner = terms[0][0].shape
    rows = rows // part[1]
    col_width = terms[-1][1].shape[1] // halves

    def w_spec(is_local, hp):
        if is_local:
            return pl.BlockSpec((inner, col_width), lambda i, m: (hp, m[0] * halves + m[1]))
        return pl.BlockSpec((inner, col_width), lambda i, m: (hp, m[1]))

    full = pl.BlockSpec((rows, col_width), lambda i, m: (part[0], 0))
    grid_spec = pltpu.PrefetchScalarGridSpec(
        num_scalar_prefetch=1,
        grid=(1,),
        in_specs=([full] if partial is not None else [])
        + [pl.BlockSpec((rows, inner), lambda i, m: (part[0], 0)) for _ in terms]
        + [w_spec(is_local, hp) for _, _, is_local, hp in terms],
        out_specs=pl.BlockSpec((rows, col_width), lambda i, m: (0, 0)),
    )
    extra = [partial] if partial is not None else []
    count = len(terms)
    return pl.pallas_call(
        functools.partial(part_kernel, count=count, has_partial=partial is not None),
        grid_spec=grid_spec,
        out_shape=jax.ShapeDtypeStruct((rows, col_width), out_dtype),
        cost_estimate=pl.CostEstimate(
            flops=2 * rows * inner * count * col_width,
            transcendentals=0,
            bytes_accessed=rows * inner * count * 2 + count * inner * col_width * 2
            + rows * col_width * (4 * len(extra) + jnp.dtype(out_dtype).itemsize),
        ),
    )(meta, *extra, *[t[0] for t in terms], *[t[1] for t in terms])


CTX = ("xl", "z", "core")
TP = ("y", "xh")


def per_device(queries, key_rows, value_rows, selection, out_weight):
    row_count, feat_width = queries.shape
    topk = selection.shape[1]
    y_size = lax.axis_size("y")
    xh_size = lax.axis_size("xh")
    y_place = lax.axis_index("y")
    ctx_place = lax.axis_index(CTX)
    own_choice = lax.dynamic_slice_in_dim(selection, ctx_place, 1, 0)[0]
    meta = jnp.concatenate([own_choice, ctx_place.astype(jnp.int32)[None]])
    kv_piece = lax.all_gather(
        jnp.concatenate([key_rows, value_rows], axis=1), CTX, axis=0, tiled=True
    )
    group_width = out_weight.shape[1] // y_size
    received = []
    for shift in range(1, y_size):
        dest = (y_place + shift) % y_size
        sent = lax.dynamic_slice_in_dim(out_weight, dest * group_width, group_width, 1)
        received.append(
            lax.ppermute(sent, "y", [(i, (i + shift) % y_size) for i in range(y_size)])
        )
    kv_piece, received = lax.optimization_barrier((kv_piece, received))
    parts = 2
    by_shift = [[] for _ in range(y_size)]
    for half in range(parts):
        attended = attend(meta, queries, kv_piece, topk, half, parts)
        by_shift[0].append(attended)
        for shift in range(1, y_size):
            by_shift[shift].append(
                lax.ppermute(attended, "y", [(i, (i + shift) % y_size) for i in range(y_size)])
            )
    weight_of = [out_weight] + list(received)

    def terms(shift):
        return [(by_shift[shift][h], weight_of[shift], shift == 0, h) for h in range(parts)]

    xh_place = lax.axis_index("xh")
    other = jnp.stack([y_place, xh_size - 1 - xh_place]).astype(jnp.int32)
    mine = jnp.stack([y_place, xh_place]).astype(jnp.int32)
    early = project_part(other, None, terms(0) + terms(1), xh_size, jnp.float32)
    near = project_part(other, early, terms(3), xh_size, jnp.float32)
    swap = [(i, xh_size - 1 - i) for i in range(xh_size)]
    got = [
        lax.ppermute(
            project_part(other, near, terms(2), xh_size, queries.dtype, (r, 2)), "xh", swap
        )
        for r in range(2)
    ]
    got = jnp.concatenate(got)
    own = project_part(
        mine, None, terms(0) + terms(1) + terms(2) + terms(3), xh_size, jnp.float32
    )
    return (own + got.astype(jnp.float32)).astype(queries.dtype)


def solution(mesh):
    ctx_size, tp_size = mesh.devices.shape
    view = Mesh(
        mesh.devices.reshape(2, ctx_size // 4, 2, tp_size // 2, 2), ("xl", "z", "core", "y", "xh")
    )
    placed = (P(CTX, TP), P(CTX, TP), P(CTX, TP), P(), P(TP, None))
    return jax.shard_map(
        per_device, mesh=view, in_specs=placed, out_specs=P(CTX, TP), check_vma=False
    )
```

```python
import functools

import jax
import jax.numpy as jnp
from jax import lax
from jax.experimental import pallas as pl
from jax.experimental.pallas import tpu as pltpu
from jax.sharding import Mesh, PartitionSpec as P

HD = 128
BLOCK = 512

neg_fill = -1e30


def attend_kernel(meta_ref, q_ref, *refs, topk, head_count):
    k_refs = refs[:topk]
    v_refs = refs[topk : 2 * topk]
    att_ref = refs[2 * topk]
    if True:
        scaling = 1.0 / jnp.sqrt(jnp.float32(HD))
        q_block = meta_ref[topk]
        query_pos = q_block * BLOCK + lax.broadcasted_iota(jnp.int32, (BLOCK, BLOCK), 0)
        key_pos = meta_ref[0] * BLOCK + lax.broadcasted_iota(jnp.int32, (BLOCK, BLOCK), 1)
        causal = key_pos <= query_pos
        usable = [None] + [
            (meta_ref[s] != meta_ref[0]) & (meta_ref[s] < q_block) for s in range(1, topk)
        ]
        for h in range(head_count):
            cols = slice(h * HD, (h + 1) * HD)
            q = q_ref[:, cols]
            scores = []
            for s in range(topk):
                sc = lax.dot_general(
                    q, k_refs[s][:, cols], (((1,), (1,)), ((), ())),
                    preferred_element_type=jnp.float32,
                ) * scaling
                if s == 0:
                    sc = jnp.where(causal, sc, neg_fill)
                else:
                    sc = jnp.where(usable[s], sc, neg_fill)
                scores.append(sc)
            row_max = jnp.max(scores[0], axis=1, keepdims=True)
            for s in range(1, topk):
                row_max = jnp.maximum(row_max, jnp.max(scores[s], axis=1, keepdims=True))
            row_sum = jnp.zeros((BLOCK, 1), jnp.float32)
            acc = jnp.zeros((BLOCK, HD), jnp.float32)
            for s in range(topk):
                e = jnp.exp(scores[s] - row_max)
                row_sum = row_sum + jnp.sum(e, axis=1, keepdims=True)
                acc = acc + jnp.dot(
                    e.astype(jnp.bfloat16), v_refs[s][:, cols],
                    preferred_element_type=jnp.float32,
                )
            att_ref[:, cols] = (acc / row_sum).astype(att_ref.dtype)


def project_kernel(y_ref, *refs, shifts):
    a_refs = refs[:shifts]
    w_refs = refs[shifts : 2 * shifts]
    o_ref = refs[2 * shifts]
    acc = jnp.dot(a_refs[0][...], w_refs[0][...], preferred_element_type=jnp.float32)
    for sh in range(1, shifts):
        acc = acc + jnp.dot(a_refs[sh][...], w_refs[sh][...], preferred_element_type=jnp.float32)
    o_ref[...] = acc.astype(o_ref.dtype)


def attend(meta, queries, kv_piece, topk):
    row_count, feat_width = queries.shape
    head_count = feat_width // HD

    def k_map(s):
        return lambda j, m: (m[s], 0)

    def v_map(s):
        return lambda j, m: (m[s], 1)

    blk = (BLOCK, feat_width)
    grid_spec = pltpu.PrefetchScalarGridSpec(
        num_scalar_prefetch=1,
        grid=(1,),
        in_specs=[pl.BlockSpec(blk, lambda j, m: (0, 0))]
        + [pl.BlockSpec(blk, k_map(s)) for s in range(topk)]
        + [pl.BlockSpec(blk, v_map(s)) for s in range(topk)],
        out_specs=pl.BlockSpec(blk, lambda j, m: (0, 0)),
    )
    return pl.pallas_call(
        functools.partial(attend_kernel, topk=topk, head_count=head_count),
        grid_spec=grid_spec,
        out_shape=jax.ShapeDtypeStruct((row_count, feat_width), queries.dtype),
        cost_estimate=pl.CostEstimate(
            flops=4 * head_count * BLOCK * topk * BLOCK * HD,
            transcendentals=head_count * BLOCK * topk * BLOCK,
            bytes_accessed=queries.size * 2 * (2 + 2 * topk),
        ),
    )(meta, queries, *([kv_piece] * (2 * topk)))


def project(meta, pieces, out_weight, received, halves, out_dtype):
    rows, inner = pieces[0].shape
    shifts = len(received) + 1
    col_width = received[0].shape[1] // halves
    grid_spec = pltpu.PrefetchScalarGridSpec(
        num_scalar_prefetch=1,
        grid=(1,),
        in_specs=[pl.BlockSpec((rows, inner), lambda i, m: (0, 0)) for _ in range(shifts)]
        + [pl.BlockSpec((inner, col_width), lambda i, m: (0, m[0] * halves + m[1]))]
        + [pl.BlockSpec((inner, col_width), lambda i, m: (0, m[1])) for _ in received],
        out_specs=pl.BlockSpec((rows, col_width), lambda i, m: (0, 0)),
    )
    return pl.pallas_call(
        functools.partial(project_kernel, shifts=shifts),
        grid_spec=grid_spec,
        out_shape=jax.ShapeDtypeStruct((rows, col_width), out_dtype),
        cost_estimate=pl.CostEstimate(
            flops=2 * rows * inner * shifts * col_width,
            transcendentals=0,
            bytes_accessed=rows * inner * shifts * 2 + shifts * inner * col_width * 2
            + rows * col_width * jnp.dtype(out_dtype).itemsize,
        ),
    )(meta, *pieces, out_weight, *received)


def part_kernel(meta_ref, *refs, count, has_partial):
    start = 1 if has_partial else 0
    a_refs = refs[start : start + count]
    w_refs = refs[start + count : start + 2 * count]
    o_ref = refs[start + 2 * count]
    acc = refs[0][...] if has_partial else None
    for a_ref, w_ref in zip(a_refs, w_refs):
        term = jnp.dot(a_ref[...], w_ref[...], preferred_element_type=jnp.float32)
        acc = term if acc is None else acc + term
    o_ref[...] = acc.astype(o_ref.dtype)


def project_part(meta, partial, pieces, weights, local_first, halves, out_dtype, part=(0, 1)):
    rows, inner = pieces[0].shape
    rows = rows // part[1]
    col_width = weights[-1].shape[1] // halves
    w_specs = [pl.BlockSpec((inner, col_width), lambda i, m: (0, m[1])) for _ in weights]
    if local_first:
        w_specs[0] = pl.BlockSpec((inner, col_width), lambda i, m: (0, m[0] * halves + m[1]))
    full = pl.BlockSpec((rows, col_width), lambda i, m: (part[0], 0))
    grid_spec = pltpu.PrefetchScalarGridSpec(
        num_scalar_prefetch=1,
        grid=(1,),
        in_specs=([full] if partial is not None else [])
        + [pl.BlockSpec((rows, inner), lambda i, m: (part[0], 0)) for _ in pieces]
        + w_specs,
        out_specs=pl.BlockSpec((rows, col_width), lambda i, m: (0, 0)),
    )
    extra = [partial] if partial is not None else []
    return pl.pallas_call(
        functools.partial(part_kernel, count=len(pieces), has_partial=partial is not None),
        grid_spec=grid_spec,
        out_shape=jax.ShapeDtypeStruct((rows, col_width), out_dtype),
        cost_estimate=pl.CostEstimate(
            flops=2 * rows * inner * len(pieces) * col_width,
            transcendentals=0,
            bytes_accessed=rows * inner * len(pieces) * 2 + len(pieces) * inner * col_width * 2
            + rows * col_width * (4 * len(extra) + jnp.dtype(out_dtype).itemsize),
        ),
    )(meta, *extra, *pieces, *weights)


CTX = ("xl", "z", "core")
TP = ("y", "xh")


def per_device(queries, key_rows, value_rows, selection, out_weight):
    row_count, feat_width = queries.shape
    topk = selection.shape[1]
    y_size = lax.axis_size("y")
    xh_size = lax.axis_size("xh")
    y_place = lax.axis_index("y")
    ctx_place = lax.axis_index(CTX)
    own_choice = lax.dynamic_slice_in_dim(selection, ctx_place, 1, 0)[0]
    meta = jnp.concatenate([own_choice, ctx_place.astype(jnp.int32)[None]])
    kv_piece = lax.all_gather(
        jnp.concatenate([key_rows, value_rows], axis=1), CTX, axis=0, tiled=True
    )
    group_width = out_weight.shape[1] // y_size
    received = []
    for shift in range(1, y_size):
        dest = (y_place + shift) % y_size
        sent = lax.dynamic_slice_in_dim(out_weight, dest * group_width, group_width, 1)
        received.append(
            lax.ppermute(sent, "y", [(i, (i + shift) % y_size) for i in range(y_size)])
        )
    kv_piece, received = lax.optimization_barrier((kv_piece, received))
    attended = attend(meta, queries, kv_piece, topk)
    pieces = [attended] + [
        lax.ppermute(attended, "y", [(i, (i + shift) % y_size) for i in range(y_size)])
        for shift in range(1, y_size)
    ]
    xh_place = lax.axis_index("xh")
    other = jnp.stack([y_place, xh_size - 1 - xh_place]).astype(jnp.int32)
    mine = jnp.stack([y_place, xh_place]).astype(jnp.int32)
    early = project_part(
        other, None, pieces[:2], [out_weight, received[0]], True, xh_size, jnp.float32
    )
    near = project_part(
        other, early, pieces[3:], list(received[2:]), False, xh_size, jnp.float32
    )
    swap = [(i, xh_size - 1 - i) for i in range(xh_size)]
    got = [
        lax.ppermute(
            project_part(
                other, near, pieces[2:3], list(received[1:2]), False, xh_size, queries.dtype,
                (r, 2),
            ),
            "xh",
            swap,
        )
        for r in range(2)
    ]
    got = jnp.concatenate(got)
    own = project(mine, pieces, out_weight, received, xh_size, queries.dtype)
    return (own.astype(jnp.float32) + got.astype(jnp.float32)).astype(queries.dtype)


def solution(mesh):
    ctx_size, tp_size = mesh.devices.shape
    view = Mesh(
        mesh.devices.reshape(2, ctx_size // 4, 2, tp_size // 2, 2), ("xl", "z", "core", "y", "xh")
    )
    placed = (P(CTX, TP), P(CTX, TP), P(CTX, TP), P(), P(TP, None))
    return jax.shard_map(
        per_device, mesh=view, in_specs=placed, out_specs=P(CTX, TP), check_vma=False
    )
```

```python
import functools

import jax
import jax.numpy as jnp
from jax import lax
from jax.experimental import pallas as pl
from jax.experimental.pallas import tpu as pltpu
from jax.sharding import Mesh, PartitionSpec as P

HD = 128
BLOCK = 512

neg_fill = -1e30


def attend_kernel(meta_ref, q_ref, *refs, topk, head_count):
    k_refs = refs[:topk]
    v_refs = refs[topk : 2 * topk]
    att_ref = refs[2 * topk]
    if True:
        scaling = 1.0 / jnp.sqrt(jnp.float32(HD))
        q_block = meta_ref[topk]
        query_pos = q_block * BLOCK + lax.broadcasted_iota(jnp.int32, (BLOCK, BLOCK), 0)
        key_pos = meta_ref[0] * BLOCK + lax.broadcasted_iota(jnp.int32, (BLOCK, BLOCK), 1)
        causal = key_pos <= query_pos
        usable = [None] + [
            (meta_ref[s] != meta_ref[0]) & (meta_ref[s] < q_block) for s in range(1, topk)
        ]
        for h in range(head_count):
            cols = slice(h * HD, (h + 1) * HD)
            q = q_ref[:, cols]
            scores = []
            for s in range(topk):
                sc = lax.dot_general(
                    q, k_refs[s][:, cols], (((1,), (1,)), ((), ())),
                    preferred_element_type=jnp.float32,
                ) * scaling
                if s == 0:
                    sc = jnp.where(causal, sc, neg_fill)
                else:
                    sc = jnp.where(usable[s], sc, neg_fill)
                scores.append(sc)
            row_max = jnp.max(scores[0], axis=1, keepdims=True)
            for s in range(1, topk):
                row_max = jnp.maximum(row_max, jnp.max(scores[s], axis=1, keepdims=True))
            row_sum = jnp.zeros((BLOCK, 1), jnp.float32)
            acc = jnp.zeros((BLOCK, HD), jnp.float32)
            for s in range(topk):
                e = jnp.exp(scores[s] - row_max)
                row_sum = row_sum + jnp.sum(e, axis=1, keepdims=True)
                acc = acc + jnp.dot(
                    e.astype(jnp.bfloat16), v_refs[s][:, cols],
                    preferred_element_type=jnp.float32,
                )
            att_ref[:, cols] = (acc / row_sum).astype(att_ref.dtype)


def project_kernel(y_ref, *refs, shifts):
    a_refs = refs[:shifts]
    w_refs = refs[shifts : 2 * shifts]
    o_ref = refs[2 * shifts]
    acc = jnp.dot(a_refs[0][...], w_refs[0][...], preferred_element_type=jnp.float32)
    for sh in range(1, shifts):
        acc = acc + jnp.dot(a_refs[sh][...], w_refs[sh][...], preferred_element_type=jnp.float32)
    o_ref[...] = acc.astype(o_ref.dtype)


def attend(meta, queries, kv_piece, topk):
    row_count, feat_width = queries.shape
    head_count = feat_width // HD

    def k_map(s):
        return lambda j, m: (m[s], 0)

    def v_map(s):
        return lambda j, m: (m[s], 1)

    blk = (BLOCK, feat_width)
    grid_spec = pltpu.PrefetchScalarGridSpec(
        num_scalar_prefetch=1,
        grid=(1,),
        in_specs=[pl.BlockSpec(blk, lambda j, m: (0, 0))]
        + [pl.BlockSpec(blk, k_map(s)) for s in range(topk)]
        + [pl.BlockSpec(blk, v_map(s)) for s in range(topk)],
        out_specs=pl.BlockSpec(blk, lambda j, m: (0, 0)),
    )
    return pl.pallas_call(
        functools.partial(attend_kernel, topk=topk, head_count=head_count),
        grid_spec=grid_spec,
        out_shape=jax.ShapeDtypeStruct((row_count, feat_width), queries.dtype),
        cost_estimate=pl.CostEstimate(
            flops=4 * head_count * BLOCK * topk * BLOCK * HD,
            transcendentals=head_count * BLOCK * topk * BLOCK,
            bytes_accessed=queries.size * 2 * (2 + 2 * topk),
        ),
    )(meta, queries, *([kv_piece] * (2 * topk)))


def project(meta, pieces, out_weight, received, halves, out_dtype):
    rows, inner = pieces[0].shape
    shifts = len(received) + 1
    col_width = received[0].shape[1] // halves
    grid_spec = pltpu.PrefetchScalarGridSpec(
        num_scalar_prefetch=1,
        grid=(1,),
        in_specs=[pl.BlockSpec((rows, inner), lambda i, m: (0, 0)) for _ in range(shifts)]
        + [pl.BlockSpec((inner, col_width), lambda i, m: (0, m[0] * halves + m[1]))]
        + [pl.BlockSpec((inner, col_width), lambda i, m: (0, m[1])) for _ in received],
        out_specs=pl.BlockSpec((rows, col_width), lambda i, m: (0, 0)),
    )
    return pl.pallas_call(
        functools.partial(project_kernel, shifts=shifts),
        grid_spec=grid_spec,
        out_shape=jax.ShapeDtypeStruct((rows, col_width), out_dtype),
        cost_estimate=pl.CostEstimate(
            flops=2 * rows * inner * shifts * col_width,
            transcendentals=0,
            bytes_accessed=rows * inner * shifts * 2 + shifts * inner * col_width * 2
            + rows * col_width * jnp.dtype(out_dtype).itemsize,
        ),
    )(meta, *pieces, out_weight, *received)


def part_kernel(meta_ref, *refs, count, has_partial):
    start = 1 if has_partial else 0
    a_refs = refs[start : start + count]
    w_refs = refs[start + count : start + 2 * count]
    o_ref = refs[start + 2 * count]
    acc = refs[0][...] if has_partial else None
    for a_ref, w_ref in zip(a_refs, w_refs):
        term = jnp.dot(a_ref[...], w_ref[...], preferred_element_type=jnp.float32)
        acc = term if acc is None else acc + term
    o_ref[...] = acc.astype(o_ref.dtype)


def project_part(meta, partial, pieces, weights, local_first, halves, out_dtype, part=(0, 1)):
    rows, inner = pieces[0].shape
    rows = rows // part[1]
    col_width = weights[-1].shape[1] // halves
    w_specs = [pl.BlockSpec((inner, col_width), lambda i, m: (0, m[1])) for _ in weights]
    if local_first:
        w_specs[0] = pl.BlockSpec((inner, col_width), lambda i, m: (0, m[0] * halves + m[1]))
    full = pl.BlockSpec((rows, col_width), lambda i, m: (part[0], 0))
    grid_spec = pltpu.PrefetchScalarGridSpec(
        num_scalar_prefetch=1,
        grid=(1,),
        in_specs=([full] if partial is not None else [])
        + [pl.BlockSpec((rows, inner), lambda i, m: (part[0], 0)) for _ in pieces]
        + w_specs,
        out_specs=pl.BlockSpec((rows, col_width), lambda i, m: (0, 0)),
    )
    extra = [partial] if partial is not None else []
    return pl.pallas_call(
        functools.partial(part_kernel, count=len(pieces), has_partial=partial is not None),
        grid_spec=grid_spec,
        out_shape=jax.ShapeDtypeStruct((rows, col_width), out_dtype),
        cost_estimate=pl.CostEstimate(
            flops=2 * rows * inner * len(pieces) * col_width,
            transcendentals=0,
            bytes_accessed=rows * inner * len(pieces) * 2 + len(pieces) * inner * col_width * 2
            + rows * col_width * (4 * len(extra) + jnp.dtype(out_dtype).itemsize),
        ),
    )(meta, *extra, *pieces, *weights)


CTX = ("xl", "z", "core")
TP = ("y", "xh")


def per_device(queries, key_rows, value_rows, selection, out_weight):
    row_count, feat_width = queries.shape
    topk = selection.shape[1]
    y_size = lax.axis_size("y")
    xh_size = lax.axis_size("xh")
    y_place = lax.axis_index("y")
    ctx_place = lax.axis_index(CTX)
    own_choice = lax.dynamic_slice_in_dim(selection, ctx_place, 1, 0)[0]
    meta = jnp.concatenate([own_choice, ctx_place.astype(jnp.int32)[None]])
    kv_piece = lax.all_gather(
        jnp.concatenate([key_rows, value_rows], axis=1), CTX, axis=0, tiled=True
    )
    group_width = out_weight.shape[1] // y_size
    received = []
    for shift in range(1, y_size):
        dest = (y_place + shift) % y_size
        sent = lax.dynamic_slice_in_dim(out_weight, dest * group_width, group_width, 1)
        received.append(
            lax.ppermute(sent, "y", [(i, (i + shift) % y_size) for i in range(y_size)])
        )
    kv_piece, received = lax.optimization_barrier((kv_piece, received))
    attended = attend(meta, queries, kv_piece, topk)
    pieces = [attended] + [
        lax.ppermute(attended, "y", [(i, (i + shift) % y_size) for i in range(y_size)])
        for shift in range(1, y_size)
    ]
    xh_place = lax.axis_index("xh")
    other = jnp.stack([y_place, xh_size - 1 - xh_place]).astype(jnp.int32)
    mine = jnp.stack([y_place, xh_place]).astype(jnp.int32)
    early = project_part(
        other, None, pieces[:2], [out_weight, received[0]], True, xh_size, jnp.float32
    )
    near = project_part(
        other, early, pieces[3:], list(received[2:]), False, xh_size, jnp.float32
    )
    swap = [(i, xh_size - 1 - i) for i in range(xh_size)]
    got = [
        lax.ppermute(
            project_part(
                other, near, pieces[2:3], list(received[1:2]), False, xh_size, queries.dtype,
                (r, 4),
            ),
            "xh",
            swap,
        )
        for r in range(4)
    ]
    got = jnp.concatenate(got)
    own = project(mine, pieces, out_weight, received, xh_size, jnp.float32)
    return (own + got.astype(jnp.float32)).astype(queries.dtype)


def solution(mesh):
    ctx_size, tp_size = mesh.devices.shape
    view = Mesh(
        mesh.devices.reshape(2, ctx_size // 4, 2, tp_size // 2, 2), ("xl", "z", "core", "y", "xh")
    )
    placed = (P(CTX, TP), P(CTX, TP), P(CTX, TP), P(), P(TP, None))
    return jax.shard_map(
        per_device, mesh=view, in_specs=placed, out_specs=P(CTX, TP), check_vma=False
    )
```

```python
import functools

import jax
import jax.numpy as jnp
from jax import lax
from jax.experimental import pallas as pl
from jax.experimental.pallas import tpu as pltpu
from jax.sharding import Mesh, PartitionSpec as P

HD = 128
BLOCK = 512

neg_fill = -1e30


def attend_kernel(meta_ref, q_ref, *refs, topk, head_count):
    k_refs = refs[:topk]
    v_refs = refs[topk : 2 * topk]
    att_ref = refs[2 * topk]
    if True:
        scaling = 1.0 / jnp.sqrt(jnp.float32(HD))
        q_block = meta_ref[topk]
        query_pos = q_block * BLOCK + lax.broadcasted_iota(jnp.int32, (BLOCK, BLOCK), 0)
        key_pos = meta_ref[0] * BLOCK + lax.broadcasted_iota(jnp.int32, (BLOCK, BLOCK), 1)
        causal = key_pos <= query_pos
        usable = [None] + [
            (meta_ref[s] != meta_ref[0]) & (meta_ref[s] < q_block) for s in range(1, topk)
        ]
        for h in range(head_count):
            cols = slice(h * HD, (h + 1) * HD)
            q = q_ref[:, cols]
            scores = []
            for s in range(topk):
                sc = lax.dot_general(
                    q, k_refs[s][:, cols], (((1,), (1,)), ((), ())),
                    preferred_element_type=jnp.float32,
                ) * scaling
                if s == 0:
                    sc = jnp.where(causal, sc, neg_fill)
                else:
                    sc = jnp.where(usable[s], sc, neg_fill)
                scores.append(sc)
            top = scores[0]
            for s in range(1, topk):
                top = jnp.maximum(top, scores[s])
            row_max = jnp.max(top, axis=1, keepdims=True)
            total = None
            acc = jnp.zeros((BLOCK, HD), jnp.float32)
            for s in range(topk):
                e = jnp.exp(scores[s] - row_max)
                total = e if total is None else total + e
                acc = acc + jnp.dot(
                    e.astype(jnp.bfloat16), v_refs[s][:, cols],
                    preferred_element_type=jnp.float32,
                )
            row_sum = jnp.sum(total, axis=1, keepdims=True)
            att_ref[:, cols] = (acc / row_sum).astype(att_ref.dtype)


def project_kernel(y_ref, *refs, shifts):
    a_refs = refs[:shifts]
    w_refs = refs[shifts : 2 * shifts]
    o_ref = refs[2 * shifts]
    acc = jnp.dot(a_refs[0][...], w_refs[0][...], preferred_element_type=jnp.float32)
    for sh in range(1, shifts):
        acc = acc + jnp.dot(a_refs[sh][...], w_refs[sh][...], preferred_element_type=jnp.float32)
    o_ref[...] = acc.astype(o_ref.dtype)


def attend(meta, queries, kv_piece, topk):
    row_count, feat_width = queries.shape
    head_count = feat_width // HD

    def k_map(s):
        return lambda j, m: (m[s], 0)

    def v_map(s):
        return lambda j, m: (m[s], 1)

    blk = (BLOCK, feat_width)
    grid_spec = pltpu.PrefetchScalarGridSpec(
        num_scalar_prefetch=1,
        grid=(1,),
        in_specs=[pl.BlockSpec(blk, lambda j, m: (0, 0))]
        + [pl.BlockSpec(blk, k_map(s)) for s in range(topk)]
        + [pl.BlockSpec(blk, v_map(s)) for s in range(topk)],
        out_specs=pl.BlockSpec(blk, lambda j, m: (0, 0)),
    )
    return pl.pallas_call(
        functools.partial(attend_kernel, topk=topk, head_count=head_count),
        grid_spec=grid_spec,
        out_shape=jax.ShapeDtypeStruct((row_count, feat_width), queries.dtype),
        cost_estimate=pl.CostEstimate(
            flops=4 * head_count * BLOCK * topk * BLOCK * HD,
            transcendentals=head_count * BLOCK * topk * BLOCK,
            bytes_accessed=queries.size * 2 * (2 + 2 * topk),
        ),
    )(meta, queries, *([kv_piece] * (2 * topk)))


def project(meta, pieces, out_weight, received, halves, out_dtype):
    rows, inner = pieces[0].shape
    shifts = len(received) + 1
    col_width = received[0].shape[1] // halves
    grid_spec = pltpu.PrefetchScalarGridSpec(
        num_scalar_prefetch=1,
        grid=(1,),
        in_specs=[pl.BlockSpec((rows, inner), lambda i, m: (0, 0)) for _ in range(shifts)]
        + [pl.BlockSpec((inner, col_width), lambda i, m: (0, m[0] * halves + m[1]))]
        + [pl.BlockSpec((inner, col_width), lambda i, m: (0, m[1])) for _ in received],
        out_specs=pl.BlockSpec((rows, col_width), lambda i, m: (0, 0)),
    )
    return pl.pallas_call(
        functools.partial(project_kernel, shifts=shifts),
        grid_spec=grid_spec,
        out_shape=jax.ShapeDtypeStruct((rows, col_width), out_dtype),
        cost_estimate=pl.CostEstimate(
            flops=2 * rows * inner * shifts * col_width,
            transcendentals=0,
            bytes_accessed=rows * inner * shifts * 2 + shifts * inner * col_width * 2
            + rows * col_width * jnp.dtype(out_dtype).itemsize,
        ),
    )(meta, *pieces, out_weight, *received)


def part_kernel(meta_ref, *refs, count, has_partial):
    start = 1 if has_partial else 0
    a_refs = refs[start : start + count]
    w_refs = refs[start + count : start + 2 * count]
    o_ref = refs[start + 2 * count]
    acc = refs[0][...] if has_partial else None
    for a_ref, w_ref in zip(a_refs, w_refs):
        term = jnp.dot(a_ref[...], w_ref[...], preferred_element_type=jnp.float32)
        acc = term if acc is None else acc + term
    o_ref[...] = acc.astype(o_ref.dtype)


def project_part(meta, partial, pieces, weights, local_first, halves, out_dtype, part=(0, 1)):
    rows, inner = pieces[0].shape
    rows = rows // part[1]
    col_width = weights[-1].shape[1] // halves
    w_specs = [pl.BlockSpec((inner, col_width), lambda i, m: (0, m[1])) for _ in weights]
    if local_first:
        w_specs[0] = pl.BlockSpec((inner, col_width), lambda i, m: (0, m[0] * halves + m[1]))
    full = pl.BlockSpec((rows, col_width), lambda i, m: (part[0], 0))
    grid_spec = pltpu.PrefetchScalarGridSpec(
        num_scalar_prefetch=1,
        grid=(1,),
        in_specs=([full] if partial is not None else [])
        + [pl.BlockSpec((rows, inner), lambda i, m: (part[0], 0)) for _ in pieces]
        + w_specs,
        out_specs=pl.BlockSpec((rows, col_width), lambda i, m: (0, 0)),
    )
    extra = [partial] if partial is not None else []
    return pl.pallas_call(
        functools.partial(part_kernel, count=len(pieces), has_partial=partial is not None),
        grid_spec=grid_spec,
        out_shape=jax.ShapeDtypeStruct((rows, col_width), out_dtype),
        cost_estimate=pl.CostEstimate(
            flops=2 * rows * inner * len(pieces) * col_width,
            transcendentals=0,
            bytes_accessed=rows * inner * len(pieces) * 2 + len(pieces) * inner * col_width * 2
            + rows * col_width * (4 * len(extra) + jnp.dtype(out_dtype).itemsize),
        ),
    )(meta, *extra, *pieces, *weights)


CTX = ("xl", "z", "core")
TP = ("y", "xh")


def per_device(queries, key_rows, value_rows, selection, out_weight):
    row_count, feat_width = queries.shape
    topk = selection.shape[1]
    y_size = lax.axis_size("y")
    xh_size = lax.axis_size("xh")
    y_place = lax.axis_index("y")
    ctx_place = lax.axis_index(CTX)
    own_choice = lax.dynamic_slice_in_dim(selection, ctx_place, 1, 0)[0]
    meta = jnp.concatenate([own_choice, ctx_place.astype(jnp.int32)[None]])
    kv_piece = lax.all_gather(
        jnp.concatenate([key_rows, value_rows], axis=1), CTX, axis=0, tiled=True
    )
    group_width = out_weight.shape[1] // y_size
    received = []
    for shift in range(1, y_size):
        dest = (y_place + shift) % y_size
        sent = lax.dynamic_slice_in_dim(out_weight, dest * group_width, group_width, 1)
        received.append(
            lax.ppermute(sent, "y", [(i, (i + shift) % y_size) for i in range(y_size)])
        )
    kv_piece, received = lax.optimization_barrier((kv_piece, received))
    attended = attend(meta, queries, kv_piece, topk)
    pieces = [attended] + [
        lax.ppermute(attended, "y", [(i, (i + shift) % y_size) for i in range(y_size)])
        for shift in range(1, y_size)
    ]
    xh_place = lax.axis_index("xh")
    other = jnp.stack([y_place, xh_size - 1 - xh_place]).astype(jnp.int32)
    mine = jnp.stack([y_place, xh_place]).astype(jnp.int32)
    early = project_part(
        other, None, pieces[:2], [out_weight, received[0]], True, xh_size, jnp.float32
    )
    near = project_part(
        other, early, pieces[3:], list(received[2:]), False, xh_size, jnp.float32
    )
    swap = [(i, xh_size - 1 - i) for i in range(xh_size)]
    got = [
        lax.ppermute(
            project_part(
                other, near, pieces[2:3], list(received[1:2]), False, xh_size, queries.dtype,
                (r, 2),
            ),
            "xh",
            swap,
        )
        for r in range(2)
    ]
    got = jnp.concatenate(got)
    own = project(mine, pieces, out_weight, received, xh_size, jnp.float32)
    return (own + got.astype(jnp.float32)).astype(queries.dtype)


def solution(mesh):
    ctx_size, tp_size = mesh.devices.shape
    view = Mesh(
        mesh.devices.reshape(2, ctx_size // 4, 2, tp_size // 2, 2), ("xl", "z", "core", "y", "xh")
    )
    placed = (P(CTX, TP), P(CTX, TP), P(CTX, TP), P(), P(TP, None))
    return jax.shard_map(
        per_device, mesh=view, in_specs=placed, out_specs=P(CTX, TP), check_vma=False
    )
```
